32 devices in a mesh: section: 2 (over core), dp: 4 (over y, x), mp: 4 (over z).
Axes of the slice: x: 2, y: 2, z: 4, core: 2. Of those that a mesh axis runs over, the one named last changes fastest.
Arguments:
- student_hidden: bfloat16 [768, 2432], P('mp'), may hold values from -20 to 20
- student_weight: float32 [2432, 64], P(('section', 'mp'), 'dp'), may hold values from -6 to 6
- student_ema: float32 [2432, 64], P(('section', 'mp'), 'dp'), may hold values from -6 to 6
- noise: bfloat16 [768, 64], P('mp'), may hold values from -6 to 6
- timesteps: int32 [8], P('mp'), may hold values from 0 to 7
- patch_embed: bfloat16 [64, 2432], replicated, may hold values from -0.75 to 0.75
- teacher_weight: bfloat16 [2, 4, 2432, 2432], P('section', None, 'mp', 'dp'), may hold values from -0.125 to 0.125
- modulation: bfloat16 [2, 4, 8, 2, 2432], P('section'), may hold values from -3 to 3
- layer_counts: int32 [2], P('section'), may hold values from 1 to 4, as said below
- feature_layers: int32 [2], replicated, may hold values from 0 to 7, as said below
- head_routes: int32 [2, 768, 1], P(None, 'mp'), may hold values from 0 to 3; in each aligned block of 192 rows (0 to 191, 192 to 383, ..., all dimensions but the last counted through in order) at most 60 rows name the same one
- head_owner: int32 [2, 4], replicated, may hold values from 0 to 3, each once within a row
- head_in: bfloat16 [2, 4, 2432, 256], P(None, 'mp'), may hold values from -0.125 to 0.125
- head_out: bfloat16 [2, 4, 256], P(None, 'mp'), may hold values from -0.375 to 0.375
Outputs:
- student_update: float32 [2432, 64], P(('section', 'mp'), 'dp')
- ema_new: float32 [2432, 64], P(('section', 'mp'), 'dp')
The draws below stay inside these ranges and needn't reach their ends.
Inputs may be any that keep to these rules, and one draw needn't show every extreme that they name: Each section runs its first layer_counts slots; some section runs all 4, some other section fewer. `feature_layers`: the first names a slot of the first section, the second a slot of the last section. `head_routes`: within the rows of one device no head is named by more than 60 rows of one tapped slot. `head_owner`: each row names every owner once.
All inputs are finite; a program needn't handle non-finite values.
Results may differ from the reference program's by a relative error of at most 0.015.
Values may be sent and summed in bfloat16 or wider, within the bound.
No kernel may reach another device: no remote copies, remote signals or barrier semaphores. Data moves between devices by JAX's collectives and lax.ppermute only.
A program may use at most 192 MiB of HBM per device.

```python
import math
import jax
import jax.numpy as jnp
import numpy as np
from jax import lax

D = 2432
LAT = 64
HH = 256
NT = 8
LMAX = 4
SAMP = 2
ROWS_DEV = 192
ROWS = 768
CAP = 60
N_SECTION = 2
N_DP = 4
N_MP = 4


def draw_layer_counts(key, part):
    full_segment = jax.random.randint(jax.random.fold_in(key, 101), (), 0, N_SECTION)
    offset_draw = jax.random.randint(jax.random.fold_in(key, 102), (), 1, N_SECTION)
    short_segment = (full_segment + offset_draw) % N_SECTION
    slot_counts = jax.random.randint(jax.random.fold_in(key, 103), (N_SECTION,), 1, LMAX + 1)
    short_count = jax.random.randint(jax.random.fold_in(key, 104), (), 1, LMAX)
    segment_ids = jnp.arange(N_SECTION)
    slot_counts = jnp.where(segment_ids == full_segment, LMAX, slot_counts)
    slot_counts = jnp.where(segment_ids == short_segment, short_count, slot_counts)
    return slot_counts.astype(jnp.int32)


def draw_feature_layers(key, part):
    chosen_slots = jax.random.randint(jax.random.fold_in(key, 21), (2,), 0, LMAX)
    return (chosen_slots + jnp.array([0, (N_SECTION - 1) * LMAX])).astype(jnp.int32)


def draw_student_hidden(key, part):
    column_pos = jnp.arange(D, dtype=jnp.float32) / (D - 1)
    values = jax.random.truncated_normal(jax.random.fold_in(key, 32), -4.0, 4.0, (ROWS, D), jnp.float32)
    column_scale = 1.0 + 4.0 * column_pos
    return (values * column_scale[None, :]).astype(jnp.bfloat16)


def with_ends(drawn, own_key, smallest, high):
    longest = drawn.shape.index(max(drawn.shape))
    spots = []
    for shift in (0, 1):
        where = [jax.random.randint(jax.random.fold_in(own_key, axis), (), 0, length) for axis, length in enumerate(drawn.shape)]
        where[longest] = (where[longest] + shift) % drawn.shape[longest]
        spots.append(tuple(where))
    return drawn.at[spots[0]].set(smallest).at[spots[1]].set(high)


def block_levels(key, extent, shards, low, largest):
    def one(axis_at, blocks):
        draws = jax.random.uniform(jax.random.fold_in(jax.random.fold_in(key, 6), axis_at), (blocks,), jnp.float32, low / len(shards), largest / len(shards))
        return jnp.repeat(jnp.exp(draws), extent[axis_at] // blocks).reshape((-1,) + (1,) * (len(extent) - axis_at - 1))

    gain = one(*shards[0])
    for cut in shards[1:]:
        gain = gain * one(*cut)
    return gain


def shared_out(stream_key, own, number, rows, number_of, top, reach, skew):
    ranking = jax.random.permutation(stream_key, number_of)
    packed, usual = load_shares(number_of, rows * top, reach, skew, True), load_shares(number_of, rows * top, reach, skew, False)
    places = jnp.arange(number_of)

    def named(sizes, turn):
        used = int((sizes > 0).sum())
        fixed = max(1, used // 4)
        passed = fixed + (places - fixed + turn * (used - fixed)) % max(1, number_of - fixed)
        return jnp.zeros((number_of,), jnp.int32).at[ranking[jnp.where(places < fixed, places, passed)]].set(jnp.asarray(sizes, jnp.int32))

    sizes = jnp.where(number % 4 == 0, named(packed, number // 4), named(usual, number - number // 4 - 1))
    mixed = jax.random.permutation(jax.random.fold_in(own, 3), number_of)
    giver, sink = mixed[0:number_of // 2 * 2:2], mixed[1:number_of // 2 * 2:2]
    room = jnp.minimum(sizes[giver] - 1, reach - sizes[sink]) // 2
    room = jnp.where((giver == ranking[0]) | (sink == ranking[0]) | (sizes[sink] == 0), 0, jnp.maximum(room, 0))
    passed = jax.random.randint(jax.random.fold_in(own, 4), (number_of // 2,), 0, 1 << 20) % (room + 1)
    sizes = sizes.at[giver].add(-passed).at[sink].add(passed)
    labels = jnp.searchsorted(jnp.cumsum(sizes), jnp.arange(rows * top), side="right").astype(jnp.int32)
    table = labels.reshape(top, rows).T
    table = table[jax.random.permutation(jax.random.fold_in(own, 1), rows)]
    turn = jax.random.randint(jax.random.fold_in(own, 2), (rows, 1), 0, top)
    return jnp.take_along_axis(table, (jnp.arange(top)[None, :] + turn) % top, axis=1)


def load_shares(number_of, total, most, lean, full):
    portions = [(1 << 20) // math.isqrt(grade ** lean) + 1 for grade in range(1, number_of + 1)]
    largest = most if full else min(most, max(-(-total // number_of), total * portions[0] // sum(portions)))
    least = 1 if total - largest >= number_of - 1 else 0
    holding, surplus = [largest] + [least] * (number_of - 1), total - largest - least * (number_of - 1)
    while surplus > 0:
        candidates = [i for i in range(1, number_of) if holding[i] < largest] or [i for i in range(1, number_of) if holding[i] < most]
        mass, remaining = sum([portions[i] for i in candidates]), surplus
        for i in candidates:
            more = min(most - holding[i], max(1, remaining * portions[i] // mass), surplus)
            holding[i] = holding[i] + more
            surplus = surplus - more
    return np.array(holding)


def scatter_about(rng, shape, scale, most, shards=(), held_as=jnp.bfloat16):
    level = block_levels(rng, shape, shards, -0.22, 0.18) if shards else 1.0
    entries = jax.random.normal(rng, shape, jnp.float32) * scale * level
    return jnp.minimum(jnp.maximum(entries, -most), most).astype(held_as)


def setup_inputs(seed: int = 0) -> dict:
    keys = jax.random.split(jax.random.key(seed), 15)
    student_hidden = draw_student_hidden(jax.random.fold_in(keys[14], 71), 0)
    student_weight = scatter_about(keys[1], (D, LAT), 1.0, 6.0, ((0, 8), (1, 4)), jnp.float32)
    student_ema = scatter_about(keys[2], (D, LAT), 1.0, 6.0, ((0, 8), (1, 4)), jnp.float32)
    noise = scatter_about(keys[3], (ROWS, LAT), 1.0, 6.0, ((0, 4),))
    timesteps = with_ends(jax.random.randint(keys[4], (N_MP * SAMP,), 0, NT), jax.random.fold_in(keys[4], 1), 0, NT - 1).astype(jnp.int32)
    patch_embed = scatter_about(keys[5], (LAT, D), LAT ** -0.5, 0.75)
    teacher_weight = scatter_about(keys[6], (N_SECTION, LMAX, D, D), D ** -0.5, 0.125, ((0, 2), (2, 4), (3, 4)))
    modulation = scatter_about(keys[7], (N_SECTION, LMAX, NT, 2, D), 0.5, 3.0, ((0, 2),))
    layer_counts = draw_layer_counts(jax.random.fold_in(keys[14], 71), 0)
    feature_layers = draw_feature_layers(jax.random.fold_in(keys[14], 71), 0)
    head_routes_keys = jax.random.split(jax.random.fold_in(keys[10], 1), 2 * ROWS // ROWS_DEV)
    head_routes_turns = jax.random.permutation(jax.random.fold_in(keys[10], 3), 2 * ROWS // ROWS_DEV)
    head_routes = jax.vmap(lambda own, number: shared_out(jax.random.fold_in(keys[10], 2), own, number, ROWS_DEV, N_MP, 1, CAP, 2))(head_routes_keys, head_routes_turns).reshape((2, ROWS, 1))
    head_owner = jax.vmap(lambda own: jax.random.permutation(own, N_MP))(jax.random.split(keys[11], 2)).reshape((2, N_MP)).astype(jnp.int32)
    head_in = scatter_about(keys[12], (2, N_MP, D, HH), D ** -0.5, 0.125, ((1, 4),))
    head_out = scatter_about(keys[13], (2, N_MP, HH), HH ** -0.5, 0.375, ((1, 4),))
    return dict(student_hidden=student_hidden, student_weight=student_weight, student_ema=student_ema, noise=noise, timesteps=timesteps, patch_embed=patch_embed, teacher_weight=teacher_weight, modulation=modulation, layer_counts=layer_counts, feature_layers=feature_layers, head_routes=head_routes, head_owner=head_owner, head_in=head_in, head_out=head_out)


norm_eps = 1e-06
ema_decay = 0.99
step_size = 0.05

def gelu_slope(values):
    return jax.vjp(jax.nn.gelu, values)[1](jnp.ones_like(values))[0]

def norm_back(normed, inverse, upstream):
    return inverse * (upstream - normed * lax.optimization_barrier(jnp.mean(upstream * normed, axis=-1, keepdims=True)))

def rounded(values):
    return lax.optimization_barrier(values.astype(jnp.bfloat16)).astype(jnp.float32)

def head_grads(features, w_first, w_second, live_mask, loss_scale):
    feat_wide = features.astype(jnp.float32)
    inverse = lax.rsqrt(lax.optimization_barrier(jnp.mean(feat_wide * feat_wide, axis=-1, keepdims=True)) + norm_eps)
    normed = feat_wide * inverse
    hidden_pre = jnp.dot(normed.astype(jnp.bfloat16), w_first, preferred_element_type=jnp.float32)
    hidden_act = jax.nn.gelu(hidden_pre).astype(jnp.bfloat16)
    logits = jnp.dot(hidden_act, w_second, preferred_element_type=jnp.float32)
    logit_grad = -loss_scale * jax.nn.sigmoid(-logits) * live_mask
    act_grad = logit_grad[:, None] * w_second.astype(jnp.float32)[None, :]
    pre_grad = (act_grad * gelu_slope(hidden_pre)).astype(jnp.bfloat16)
    normed_grad = jnp.dot(pre_grad, w_first.T, preferred_element_type=jnp.float32)
    return norm_back(normed, inverse, normed_grad).astype(jnp.bfloat16)

def route_tap(features, routes, owners_map, w_first_all, w_second_all, loss_scale):
    total_rows = features.shape[0]
    owner_ids = owners_map[routes]
    row_order = jnp.argsort(owner_ids, stable=True).astype(jnp.int32)
    owner_hot = (owner_ids[:, None] == jnp.arange(N_MP, dtype=jnp.int32)[None, :]).astype(jnp.int32)
    counts = lax.optimization_barrier(jnp.sum(owner_hot, axis=0))
    starts = jnp.cumsum(counts) - counts
    sorted_feat = features[row_order]
    sorted_owner = owner_ids[row_order]
    buffer_rows = N_MP * CAP

    def per_owner(owner_id):
        local_ids = jnp.arange(buffer_rows, dtype=jnp.int32)
        places = starts[owner_id] + local_ids
        live_rows = (local_ids < counts[owner_id]).astype(jnp.float32)
        picked = sorted_feat[jnp.clip(places, 0, total_rows - 1)]
        return head_grads(picked, w_first_all[owner_id], w_second_all[owner_id], live_rows, loss_scale)
    results = lax.map(per_owner, jnp.arange(N_MP, dtype=jnp.int32))
    within = jnp.arange(total_rows, dtype=jnp.int32) - starts[sorted_owner]
    sorted_grad = results[sorted_owner, within]
    return jnp.zeros_like(features).at[row_order].set(sorted_grad)

def reference(student_hidden, student_weight, student_ema, noise, timesteps, patch_embed, teacher_weight, modulation, layer_counts, feature_layers, head_routes, head_owner, head_in, head_out):
    total_rows = student_hidden.shape[0]
    t_rows = jnp.repeat(timesteps, ROWS_DEV // SAMP)
    noise_level = ((t_rows + 1).astype(jnp.float32) / (NT + 1))[:, None]
    latents = (jnp.dot(student_hidden, student_weight.astype(jnp.bfloat16), preferred_element_type=jnp.float32) * D ** (-0.5)).astype(jnp.bfloat16)
    noisy_input = ((1.0 - noise_level) * latents.astype(jnp.float32) + noise_level * noise.astype(jnp.float32)).astype(jnp.bfloat16)
    stream = jnp.dot(noisy_input, patch_embed, preferred_element_type=jnp.float32)
    saved_layers = []
    tap_features = [jnp.zeros((total_rows, D), jnp.bfloat16), jnp.zeros((total_rows, D), jnp.bfloat16)]
    for segment_no in range(N_SECTION):
        for slot_no in range(LMAX):
            layer_no = segment_no * LMAX + slot_no
            active = (slot_no < layer_counts[segment_no]).astype(jnp.float32)
            mod_table = modulation[segment_no, slot_no].astype(jnp.float32)[t_rows]
            scale_rows = mod_table[:, 0]
            gate_rows = mod_table[:, 1]
            inverse = lax.rsqrt(lax.optimization_barrier(jnp.mean(stream * stream, axis=-1, keepdims=True)) + norm_eps)
            normed_in = (stream * inverse * (1.0 + scale_rows)).astype(jnp.bfloat16)
            pre_act = jnp.dot(normed_in, teacher_weight[segment_no, slot_no], preferred_element_type=jnp.float32)
            slot_out = (active * gate_rows * jax.nn.gelu(pre_act)).astype(jnp.bfloat16)
            saved_layers.append((stream, inverse, scale_rows, gate_rows, active, pre_act))
            stream = stream + slot_out.astype(jnp.float32)
            for tap_no in range(2):
                tap_features[tap_no] = jnp.where(feature_layers[tap_no] == layer_no, stream.astype(jnp.bfloat16), tap_features[tap_no])
        if segment_no + 1 < N_SECTION:
            stream = rounded(stream)
    loss_scale = D / math.sqrt(total_rows)
    tap_grads = [route_tap(tap_features[tap_no], head_routes[tap_no, :, 0], head_owner[tap_no], head_in[tap_no], head_out[tap_no], loss_scale) for tap_no in range(2)]
    col_width = D // N_DP
    grad_stream = jnp.zeros((total_rows, D), jnp.float32)
    for segment_no in reversed(range(N_SECTION)):
        for slot_no in reversed(range(LMAX)):
            layer_no = segment_no * LMAX + slot_no
            for tap_no in range(2):
                grad_stream = grad_stream + jnp.where(feature_layers[tap_no] == layer_no, tap_grads[tap_no].astype(jnp.float32), 0.0)
            stream_in, inverse, scale_rows, gate_rows, active, pre_act = saved_layers[layer_no]
            pre_grad = (grad_stream * active * gate_rows * gelu_slope(pre_act)).astype(jnp.bfloat16)
            weight_now = teacher_weight[segment_no, slot_no]
            input_grad = jnp.zeros((total_rows, D), jnp.float32)
            for part_no in range(N_DP):
                lower = part_no * col_width
                partial_grad = jnp.dot(pre_grad[:, lower:lower + col_width], weight_now[:, lower:lower + col_width].T, preferred_element_type=jnp.float32)
                input_grad = input_grad + rounded(partial_grad)
            grad_stream = grad_stream + norm_back(stream_in * inverse, inverse, input_grad * (1.0 + scale_rows))
        if segment_no > 0:
            grad_stream = rounded(grad_stream)
    latent_pre = jnp.dot(grad_stream.astype(jnp.bfloat16), patch_embed.T, preferred_element_type=jnp.float32)
    latent_grad = ((1.0 - noise_level) * latent_pre).astype(jnp.bfloat16)
    student_grad = lax.dot_general(student_hidden, latent_grad, (((0,), (0,)), ((), ())), preferred_element_type=jnp.float32) * D ** (-0.5)
    mean_square = jnp.mean(student_grad * student_grad)
    student_update = student_grad * lax.rsqrt(mean_square + norm_eps)
    ema_new = ema_decay * student_ema + (1.0 - ema_decay) * (student_weight - step_size * student_update)
    return (student_update, ema_new)
```

```python
import math

import jax
import jax.numpy as jnp
from jax import lax
from jax.sharding import PartitionSpec as P

D = 2432
LAT = 64


norm_eps = 1e-06
ema_decay = 0.99
step_size = 0.05


def xor_pairs(n, d, base=0):
    return [(base + i, base + (i ^ d)) for i in range(n)]


def swap(x, axis, n, d, base=0):
    return lax.ppermute(x, axis, xor_pairs(n, d, base))


def gather_in_order(x, axis, n, me, base=0):
    parts = [x] + [swap(x, axis, n, d, base) for d in range(1, n)]
    stacked = jnp.stack(parts)
    return jnp.take(stacked, me ^ jnp.arange(n, dtype=jnp.int32), axis=0)


def gelu_slope(values):
    return jax.vjp(jax.nn.gelu, values)[1](jnp.ones_like(values))[0]


def norm_back(normed, inverse, upstream):
    return inverse * (upstream - normed * jnp.mean(upstream * normed, axis=-1, keepdims=True))


def head_grads(features, w_first, w_second, loss_scale):
    feat_wide = features.astype(jnp.float32)
    inverse = lax.rsqrt(jnp.mean(feat_wide * feat_wide, axis=-1, keepdims=True) + norm_eps)
    normed = feat_wide * inverse
    hidden_pre = jnp.dot(normed.astype(jnp.bfloat16), w_first, preferred_element_type=jnp.float32)
    hidden_act = jax.nn.gelu(hidden_pre).astype(jnp.bfloat16)
    logits = jnp.dot(hidden_act, w_second, preferred_element_type=jnp.float32)
    logit_grad = -loss_scale * jax.nn.sigmoid(-logits)
    act_grad = logit_grad[:, None] * w_second.astype(jnp.float32)[None, :]
    pre_grad = (act_grad * gelu_slope(hidden_pre)).astype(jnp.bfloat16)
    normed_grad = jnp.dot(pre_grad, w_first.T, preferred_element_type=jnp.float32)
    return norm_back(normed, inverse, normed_grad).astype(jnp.bfloat16)


def on_device(
    student_hidden,
    student_weight,
    student_ema,
    noise,
    timesteps,
    patch_embed,
    teacher_weight,
    modulation,
    layer_counts,
    feature_layers,
    head_routes,
    head_owner,
    head_in,
    head_out,
):
    row_count, width = student_hidden.shape
    n_sec = lax.axis_size("section")
    n_mp = lax.axis_size("mp")
    n_dp = lax.axis_size("dp")
    sec = lax.axis_index("section")
    me_dp = lax.axis_index("dp")
    me_mp = lax.axis_index("mp")
    slot_count = teacher_weight.shape[1]
    levels = modulation.shape[2]
    col_width = width // n_dp
    samples = timesteps.shape[0]
    per_sample = row_count // samples

    t_rows = jnp.repeat(timesteps, per_sample)
    noise_level = ((t_rows + 1).astype(jnp.float32) / (levels + 1))[:, None]

    w_cols = gather_in_order(student_weight.astype(jnp.bfloat16), "dp", n_dp, me_dp)
    w_cols = jnp.concatenate(list(w_cols), axis=1)
    row_axes = ("section", "mp")
    row_me = sec * n_mp + me_mp
    w_rows = gather_in_order(w_cols, row_axes, n_sec * n_mp, row_me)
    student_full = w_rows.reshape(width, -1)
    latents = (
        jnp.dot(student_hidden, student_full, preferred_element_type=jnp.float32) * width ** (-0.5)
    ).astype(jnp.bfloat16)
    noisy_input = (
        (1.0 - noise_level) * latents.astype(jnp.float32) + noise_level * noise.astype(jnp.float32)
    ).astype(jnp.bfloat16)
    start_stream = jnp.dot(noisy_input, patch_embed, preferred_element_type=jnp.float32)

    weights = lax.all_gather(teacher_weight[0], "mp", axis=1, tiled=True)

    mod_pick = jnp.take(modulation[0], timesteps, axis=1).astype(jnp.float32)
    mod_rows = jnp.repeat(mod_pick, per_sample, axis=1)
    scale_rows = mod_rows[:, :, 0, :]
    gate_cols = lax.dynamic_slice_in_dim(mod_rows[:, :, 1, :], me_dp * col_width, col_width, 2)
    active = (jnp.arange(slot_count, dtype=jnp.int32) < layer_counts[0]).astype(jnp.float32)

    saved = []
    taps = []
    stream = start_stream
    for tick in range(n_sec):
        tick_saved = []
        tap = jnp.zeros((row_count, width), jnp.bfloat16)
        for slot_no in range(slot_count):
            inverse = lax.rsqrt(jnp.mean(stream * stream, axis=-1, keepdims=True) + norm_eps)
            normed = stream * inverse
            normed_in = (normed * (1.0 + scale_rows[slot_no])).astype(jnp.bfloat16)
            pre_act = jnp.dot(normed_in, weights[slot_no], preferred_element_type=jnp.float32)
            tick_saved.append((normed, inverse, pre_act))
            part_out = (active[slot_no] * gate_cols[slot_no] * jax.nn.gelu(pre_act)).astype(
                jnp.bfloat16
            )
            joined = gather_in_order(
                part_out, ("section", "dp"), n_dp, me_dp, base=tick * n_dp
            )
            joined = jnp.concatenate(list(joined), axis=1)
            stream = stream + joined.astype(jnp.float32)
            hit = feature_layers[tick] == tick * slot_count + slot_no
            tap = jnp.where(hit, stream.astype(jnp.bfloat16), tap)
        saved.append(tick_saved)
        taps.append(tap)
        if tick + 1 < n_sec:
            sent = lax.ppermute(stream.astype(jnp.bfloat16), "section", [(tick, tick + 1)])
            stream = sent.astype(jnp.float32)

    tap_store = taps[0]
    for tick in range(1, n_sec):
        tap_store = jnp.where(sec == tick, taps[tick], tap_store)
    capacity = 5 * row_count // (4 * n_mp)
    owner_range = jnp.arange(n_mp, dtype=jnp.int32)
    routes = lax.dynamic_index_in_dim(head_routes[:, :, 0], sec, 0, keepdims=False)
    owners_map = lax.dynamic_index_in_dim(head_owner, sec, 0, keepdims=False)
    route_hot = (routes[:, None] == owner_range[None, :]).astype(jnp.int32)
    owner_ids = jnp.sum(route_hot * owners_map[None, :], axis=1)
    owner_hot = (owner_ids[:, None] == owner_range[None, :]).astype(jnp.int32)
    position = jnp.sum(owner_hot * (jnp.cumsum(owner_hot, axis=0) - 1), axis=1)
    target = owner_ids * capacity + position
    dispatch = (
        target[:, None] == jnp.arange(n_mp * capacity, dtype=jnp.int32)[None, :]
    ).astype(jnp.bfloat16)
    send_feat = (
        jnp.dot(dispatch.T, tap_store, preferred_element_type=jnp.float32)
        .astype(jnp.bfloat16)
        .reshape(n_mp, capacity, width)
    )
    items = [lax.dynamic_index_in_dim(send_feat, me_mp, 0, keepdims=False)]
    for d in range(1, n_mp):
        outgoing = lax.dynamic_index_in_dim(send_feat, me_mp ^ d, 0, keepdims=False)
        items.append(swap(outgoing, "mp", n_mp, d))
    loss_scale = width / math.sqrt(row_count * n_mp)
    w_first = lax.dynamic_index_in_dim(head_in[:, 0], sec, 0, keepdims=False)
    w_second = lax.dynamic_index_in_dim(head_out[:, 0], sec, 0, keepdims=False)
    head_result = head_grads(
        jnp.concatenate(items, axis=0), w_first, w_second, loss_scale
    ).reshape(n_mp, capacity, width)
    head_cols = lax.dynamic_slice_in_dim(head_result, me_dp * col_width, col_width, 2)
    back = [head_cols[0]] + [swap(head_cols[d], "mp", n_mp, d) for d in range(1, n_mp)]
    by_owner = jnp.take(jnp.stack(back), me_mp ^ owner_range, axis=0)
    tap_grads = jnp.dot(
        dispatch, by_owner.reshape(n_mp * capacity, col_width), preferred_element_type=jnp.float32
    )

    my_cols = lambda x: lax.dynamic_slice_in_dim(x, me_dp * col_width, col_width, x.ndim - 1)
    grad_stream = jnp.zeros((row_count, col_width), jnp.float32)
    for tick in range(n_sec):
        live = n_sec - 1 - tick
        tick_saved = saved[live]
        for slot_no in reversed(range(slot_count)):
            hit = feature_layers[live] == live * slot_count + slot_no
            grad_stream = grad_stream + jnp.where(hit, tap_grads, 0.0)
            normed, inverse, pre_act = tick_saved[slot_no]
            pre_grad = (
                grad_stream * active[slot_no] * gate_cols[slot_no] * gelu_slope(pre_act)
            ).astype(jnp.bfloat16)
            partial = jnp.dot(
                pre_grad, weights[slot_no].T, preferred_element_type=jnp.float32
            ).astype(jnp.bfloat16)
            partial = lax.optimization_barrier(partial)
            scaled = 1.0 + scale_rows[slot_no]
            row_term = jnp.sum(partial.astype(jnp.float32) * scaled * normed, axis=-1)
            pieces = [my_cols(partial)]
            terms = [row_term[None, :]]
            for d in range(1, n_dp):
                block = lax.dynamic_slice_in_dim(partial, (me_dp ^ d) * col_width, col_width, 1)
                pairs = xor_pairs(n_dp, d, live * n_dp)
                pieces.append(lax.ppermute(block, ("section", "dp"), pairs))
                terms.append(lax.ppermute(row_term[None, :], ("section", "dp"), pairs))
            order = me_dp ^ jnp.arange(n_dp, dtype=jnp.int32)
            ordered = jnp.take(jnp.stack(pieces), order, axis=0).astype(jnp.float32)
            term_rows = jnp.take(jnp.concatenate(terms, axis=0), order, axis=0)
            input_grad = jnp.zeros((row_count, col_width), jnp.float32)
            row_sum = jnp.zeros((row_count,), jnp.float32)
            for src in range(n_dp):
                input_grad = input_grad + ordered[src]
                row_sum = row_sum + term_rows[src]
            row_mean = (row_sum / width)[:, None]
            grad_stream = grad_stream + inverse * (
                input_grad * my_cols(scaled) - my_cols(normed) * row_mean
            )
        if tick + 1 < n_sec:
            sent = lax.ppermute(
                grad_stream.astype(jnp.bfloat16), "section", [(live, live - 1)]
            )
            grad_stream = sent.astype(jnp.float32)

    lat_part = student_weight.shape[1]
    latent_pre = jnp.dot(
        grad_stream.astype(jnp.bfloat16), my_cols(patch_embed).T, preferred_element_type=jnp.float32
    )
    got = [lax.dynamic_slice_in_dim(latent_pre, me_dp * lat_part, lat_part, 1)]
    for d in range(1, n_dp):
        block = lax.dynamic_slice_in_dim(latent_pre, (me_dp ^ d) * lat_part, lat_part, 1)
        got.append(lax.ppermute(block, ("section", "dp"), xor_pairs(n_dp, d, 0)))
    got = jnp.take(jnp.stack(got), me_dp ^ jnp.arange(n_dp, dtype=jnp.int32), axis=0)
    lat_sum = got[0]
    for src in range(1, n_dp):
        lat_sum = lat_sum + got[src]
    my_latent = ((1.0 - noise_level) * lat_sum).astype(jnp.bfloat16)
    if n_sec > 1:
        spread = lax.ppermute(my_latent, "section", [(0, s) for s in range(1, n_sec)])
        my_latent = jnp.where(sec == 0, my_latent, spread)

    own_rows = student_weight.shape[0]
    segment_block = width // n_sec
    hidden_cols = lax.dynamic_slice_in_dim(student_hidden, sec * segment_block, segment_block, 1)
    part_grad = lax.dot_general(
        hidden_cols, my_latent, (((0,), (0,)), ((), ())), preferred_element_type=jnp.float32
    ).reshape(n_mp, own_rows, lat_part)
    got = [lax.dynamic_index_in_dim(part_grad, me_mp, 0, keepdims=False)]
    for d in range(1, n_mp):
        outgoing = lax.dynamic_index_in_dim(part_grad, me_mp ^ d, 0, keepdims=False)
        got.append(swap(outgoing, "mp", n_mp, d))
    got = jnp.take(jnp.stack(got), me_mp ^ jnp.arange(n_mp, dtype=jnp.int32), axis=0)
    grad_sum = got[0]
    for src in range(1, n_mp):
        grad_sum = grad_sum + got[src]
    student_grad = grad_sum * width ** (-0.5)

    local_sq = jnp.sum(student_grad * student_grad).reshape(1)
    sq = gather_in_order(local_sq, "section", n_sec, sec).reshape(-1)
    sq = gather_in_order(sq, "dp", n_dp, me_dp).reshape(-1)
    sq = gather_in_order(sq, "mp", n_mp, me_mp).reshape(-1)
    total_sq = jnp.sum(sq)
    mean_square = total_sq / (width * LAT)
    student_update = student_grad * lax.rsqrt(mean_square + norm_eps)
    ema_new = ema_decay * student_ema + (1.0 - ema_decay) * (
        student_weight - step_size * student_update
    )
    return (student_update, ema_new)


def solution(mesh):
    in_specs = (
        P("mp", None),
        P(("section", "mp"), "dp"),
        P(("section", "mp"), "dp"),
        P("mp", None),
        P("mp"),
        P(),
        P("section", None, "mp", "dp"),
        P("section", None, None, None, None),
        P("section"),
        P(),
        P(None, "mp", None),
        P(),
        P(None, "mp", None, None),
        P(None, "mp", None),
    )
    out_specs = (P(("section", "mp"), "dp"), P(("section", "mp"), "dp"))
    return jax.shard_map(
        on_device, mesh=mesh, in_specs=in_specs, out_specs=out_specs, check_vma=False
    )
```

```python
import math

import jax
import jax.numpy as jnp
from jax import lax
from jax.sharding import PartitionSpec as P

D = 2432
LAT = 64


norm_eps = 1e-06
ema_decay = 0.99
step_size = 0.05


def xor_pairs(n, d, base=0):
    return [(base + i, base + (i ^ d)) for i in range(n)]


def swap(x, axis, n, d, base=0):
    return lax.ppermute(x, axis, xor_pairs(n, d, base))


def gather_in_order(x, axis, n, me, base=0):
    parts = [x] + [swap(x, axis, n, d, base) for d in range(1, n)]
    stacked = jnp.stack(parts)
    return jnp.take(stacked, me ^ jnp.arange(n, dtype=jnp.int32), axis=0)


def relative_blocks(x, axis, n, me):
    width = x.shape[axis] // n
    return jnp.concatenate(
        [lax.dynamic_slice_in_dim(x, (me ^ d) * width, width, axis) for d in range(n)], axis=axis
    )


def gelu_slope(values):
    return jax.vjp(jax.nn.gelu, values)[1](jnp.ones_like(values))[0]


def norm_back(normed, inverse, upstream):
    return inverse * (upstream - normed * jnp.mean(upstream * normed, axis=-1, keepdims=True))


def head_grads(features, w_first, w_second, loss_scale):
    feat_wide = features.astype(jnp.float32)
    inverse = lax.rsqrt(jnp.mean(feat_wide * feat_wide, axis=-1, keepdims=True) + norm_eps)
    normed = feat_wide * inverse
    hidden_pre = jnp.dot(normed.astype(jnp.bfloat16), w_first, preferred_element_type=jnp.float32)
    hidden_act = jax.nn.gelu(hidden_pre).astype(jnp.bfloat16)
    logits = jnp.dot(hidden_act, w_second, preferred_element_type=jnp.float32)
    logit_grad = -loss_scale * jax.nn.sigmoid(-logits)
    act_grad = logit_grad[:, None] * w_second.astype(jnp.float32)[None, :]
    pre_grad = (act_grad * gelu_slope(hidden_pre)).astype(jnp.bfloat16)
    normed_grad = jnp.dot(pre_grad, w_first.T, preferred_element_type=jnp.float32)
    return norm_back(normed, inverse, normed_grad).astype(jnp.bfloat16)


def on_device(
    student_hidden,
    student_weight,
    student_ema,
    noise,
    timesteps,
    patch_embed,
    teacher_weight,
    modulation,
    layer_counts,
    feature_layers,
    head_routes,
    head_owner,
    head_in,
    head_out,
):
    row_count, width = student_hidden.shape
    n_sec = lax.axis_size("section")
    n_mp = lax.axis_size("mp")
    n_dp = lax.axis_size("dp")
    sec = lax.axis_index("section")
    me_dp = lax.axis_index("dp")
    me_mp = lax.axis_index("mp")
    slot_count = teacher_weight.shape[1]
    levels = modulation.shape[2]
    col_width = width // n_dp
    samples = timesteps.shape[0]
    per_sample = row_count // samples

    t_rows = jnp.repeat(timesteps, per_sample)
    noise_level = ((t_rows + 1).astype(jnp.float32) / (levels + 1))[:, None]

    w_cols = gather_in_order(student_weight.astype(jnp.bfloat16), "dp", n_dp, me_dp)
    w_cols = jnp.concatenate(list(w_cols), axis=1)
    row_axes = ("section", "mp")
    row_me = sec * n_mp + me_mp
    w_rows = gather_in_order(w_cols, row_axes, n_sec * n_mp, row_me)
    student_full = w_rows.reshape(width, -1)
    latents = (
        jnp.dot(student_hidden, student_full, preferred_element_type=jnp.float32) * width ** (-0.5)
    ).astype(jnp.bfloat16)
    noisy_input = (
        (1.0 - noise_level) * latents.astype(jnp.float32) + noise_level * noise.astype(jnp.float32)
    ).astype(jnp.bfloat16)
    embed_rel = relative_blocks(patch_embed, 1, n_dp, me_dp)
    start_stream = jnp.dot(noisy_input, embed_rel, preferred_element_type=jnp.float32)

    weights = [
        relative_blocks(
            lax.all_gather(teacher_weight[0, slot_no], "mp", axis=0, tiled=True), 0, n_dp, me_dp
        )
        for slot_no in range(teacher_weight.shape[1])
    ]

    mod_pick = jnp.take(modulation[0], timesteps, axis=1).astype(jnp.float32)
    mod_rows = jnp.repeat(mod_pick, per_sample, axis=1)
    scale_rows = relative_blocks(mod_rows[:, :, 0, :], 2, n_dp, me_dp)
    gate_cols = lax.dynamic_slice_in_dim(mod_rows[:, :, 1, :], me_dp * col_width, col_width, 2)
    active = (jnp.arange(slot_count, dtype=jnp.int32) < layer_counts[0]).astype(jnp.float32)

    saved = []
    taps = []
    stream = start_stream
    for tick in range(n_sec):
        tick_saved = []
        tap = jnp.zeros((row_count, width), jnp.bfloat16)
        for slot_no in range(slot_count):
            inverse = lax.rsqrt(jnp.mean(stream * stream, axis=-1, keepdims=True) + norm_eps)
            normed = stream * inverse
            normed_in = (normed * (1.0 + scale_rows[slot_no])).astype(jnp.bfloat16)
            pre_act = jnp.dot(normed_in, weights[slot_no], preferred_element_type=jnp.float32)
            tick_saved.append((normed, inverse, pre_act))
            part_out = (active[slot_no] * gate_cols[slot_no] * jax.nn.gelu(pre_act)).astype(
                jnp.bfloat16
            )
            joined = [part_out] + [
                swap(part_out, ("section", "dp"), n_dp, d, base=tick * n_dp) for d in range(1, n_dp)
            ]
            joined = jnp.concatenate(joined, axis=1)
            stream = stream + joined.astype(jnp.float32)
            hit = feature_layers[tick] == tick * slot_count + slot_no
            tap = jnp.where(hit, stream.astype(jnp.bfloat16), tap)
        saved.append(tick_saved)
        taps.append(tap)
        if tick + 1 < n_sec:
            sent = lax.ppermute(stream.astype(jnp.bfloat16), "section", [(tick, tick + 1)])
            stream = sent.astype(jnp.float32)

    tap_store = taps[0]
    for tick in range(1, n_sec):
        tap_store = jnp.where(sec == tick, taps[tick], tap_store)
    capacity = 5 * row_count // (4 * n_mp)
    owner_range = jnp.arange(n_mp, dtype=jnp.int32)
    routes = lax.dynamic_index_in_dim(head_routes[:, :, 0], sec, 0, keepdims=False)
    owners_map = lax.dynamic_index_in_dim(head_owner, sec, 0, keepdims=False)
    route_hot = (routes[:, None] == owner_range[None, :]).astype(jnp.int32)
    owner_ids = jnp.sum(route_hot * owners_map[None, :], axis=1)
    owner_hot = (owner_ids[:, None] == owner_range[None, :]).astype(jnp.int32)
    position = jnp.sum(owner_hot * (jnp.cumsum(owner_hot, axis=0) - 1), axis=1)
    target = owner_ids * capacity + position
    dispatch = (
        target[:, None] == jnp.arange(n_mp * capacity, dtype=jnp.int32)[None, :]
    ).astype(jnp.bfloat16)
    send_feat = (
        jnp.dot(dispatch.T, tap_store, preferred_element_type=jnp.float32)
        .astype(jnp.bfloat16)
        .reshape(n_mp, capacity, width)
    )
    items = [lax.dynamic_index_in_dim(send_feat, me_mp, 0, keepdims=False)]
    for d in range(1, n_mp):
        outgoing = lax.dynamic_index_in_dim(send_feat, me_mp ^ d, 0, keepdims=False)
        items.append(swap(outgoing, "mp", n_mp, d))
    loss_scale = width / math.sqrt(row_count * n_mp)
    w_first = relative_blocks(
        lax.dynamic_index_in_dim(head_in[:, 0], sec, 0, keepdims=False), 0, n_dp, me_dp
    )
    w_second = lax.dynamic_index_in_dim(head_out[:, 0], sec, 0, keepdims=False)
    head_result = head_grads(
        jnp.concatenate(items, axis=0), w_first, w_second, loss_scale
    ).reshape(n_mp, capacity, width)
    head_cols = head_result[:, :, :col_width]
    back = [head_cols[0]] + [swap(head_cols[d], "mp", n_mp, d) for d in range(1, n_mp)]
    by_owner = jnp.take(jnp.stack(back), me_mp ^ owner_range, axis=0)
    tap_grads = jnp.dot(
        dispatch, by_owner.reshape(n_mp * capacity, col_width), preferred_element_type=jnp.float32
    )

    my_cols = lambda x: x[..., :col_width]
    grad_stream = jnp.zeros((row_count, col_width), jnp.float32)
    for tick in range(n_sec):
        live = n_sec - 1 - tick
        tick_saved = saved[live]
        for slot_no in reversed(range(slot_count)):
            hit = feature_layers[live] == live * slot_count + slot_no
            grad_stream = grad_stream + jnp.where(hit, tap_grads, 0.0)
            normed, inverse, pre_act = tick_saved[slot_no]
            pre_grad = (
                grad_stream * active[slot_no] * gate_cols[slot_no] * gelu_slope(pre_act)
            ).astype(jnp.bfloat16)
            partial = jnp.dot(
                pre_grad, weights[slot_no].T, preferred_element_type=jnp.float32
            ).astype(jnp.bfloat16)
            partial = lax.optimization_barrier(partial)
            scaled = 1.0 + scale_rows[slot_no]
            row_term = jnp.sum(partial.astype(jnp.float32) * scaled * normed, axis=-1)
            pieces = [my_cols(partial)]
            terms = [row_term[None, :]]
            for d in range(1, n_dp):
                block = partial[:, d * col_width:(d + 1) * col_width]
                pairs = xor_pairs(n_dp, d, live * n_dp)
                pieces.append(lax.ppermute(block, ("section", "dp"), pairs))
                terms.append(lax.ppermute(row_term[None, :], ("section", "dp"), pairs))
            ordered = jnp.stack(pieces).astype(jnp.float32)
            term_rows = jnp.concatenate(terms, axis=0)
            input_grad = jnp.zeros((row_count, col_width), jnp.float32)
            row_sum = jnp.zeros((row_count,), jnp.float32)
            for src in range(n_dp):
                input_grad = input_grad + ordered[src]
                row_sum = row_sum + term_rows[src]
            row_mean = (row_sum / width)[:, None]
            grad_stream = grad_stream + inverse * (
                input_grad * my_cols(scaled) - my_cols(normed) * row_mean
            )
        if tick + 1 < n_sec:
            sent = lax.ppermute(
                grad_stream.astype(jnp.bfloat16), "section", [(live, live - 1)]
            )
            grad_stream = sent.astype(jnp.float32)

    lat_part = student_weight.shape[1]
    latent_pre = jnp.dot(
        grad_stream.astype(jnp.bfloat16),
        lax.dynamic_slice_in_dim(patch_embed, me_dp * col_width, col_width, 1).T,
        preferred_element_type=jnp.float32,
    )
    got = [lax.dynamic_slice_in_dim(latent_pre, me_dp * lat_part, lat_part, 1)]
    for d in range(1, n_dp):
        block = lax.dynamic_slice_in_dim(latent_pre, (me_dp ^ d) * lat_part, lat_part, 1)
        got.append(lax.ppermute(block, ("section", "dp"), xor_pairs(n_dp, d, 0)))
    got = jnp.take(jnp.stack(got), me_dp ^ jnp.arange(n_dp, dtype=jnp.int32), axis=0)
    lat_sum = got[0]
    for src in range(1, n_dp):
        lat_sum = lat_sum + got[src]
    my_latent = ((1.0 - noise_level) * lat_sum).astype(jnp.bfloat16)
    if n_sec > 1:
        spread = lax.ppermute(my_latent, "section", [(0, s) for s in range(1, n_sec)])
        my_latent = jnp.where(sec == 0, my_latent, spread)

    own_rows = student_weight.shape[0]
    segment_block = width // n_sec
    hidden_cols = lax.dynamic_slice_in_dim(student_hidden, sec * segment_block, segment_block, 1)
    part_grad = lax.dot_general(
        hidden_cols, my_latent, (((0,), (0,)), ((), ())), preferred_element_type=jnp.float32
    ).reshape(n_mp, own_rows, lat_part)
    got = [lax.dynamic_index_in_dim(part_grad, me_mp, 0, keepdims=False)]
    for d in range(1, n_mp):
        outgoing = lax.dynamic_index_in_dim(part_grad, me_mp ^ d, 0, keepdims=False)
        got.append(swap(outgoing, "mp", n_mp, d))
    got = jnp.take(jnp.stack(got), me_mp ^ jnp.arange(n_mp, dtype=jnp.int32), axis=0)
    grad_sum = got[0]
    for src in range(1, n_mp):
        grad_sum = grad_sum + got[src]
    student_grad = grad_sum * width ** (-0.5)

    local_sq = jnp.sum(student_grad * student_grad).reshape(1)
    sq = gather_in_order(local_sq, "section", n_sec, sec).reshape(-1)
    sq = gather_in_order(sq, "dp", n_dp, me_dp).reshape(-1)
    sq = gather_in_order(sq, "mp", n_mp, me_mp).reshape(-1)
    total_sq = jnp.sum(sq)
    mean_square = total_sq / (width * LAT)
    student_update = student_grad * lax.rsqrt(mean_square + norm_eps)
    ema_new = ema_decay * student_ema + (1.0 - ema_decay) * (
        student_weight - step_size * student_update
    )
    return (student_update, ema_new)


def solution(mesh):
    in_specs = (
        P("mp", None),
        P(("section", "mp"), "dp"),
        P(("section", "mp"), "dp"),
        P("mp", None),
        P("mp"),
        P(),
        P("section", None, "mp", "dp"),
        P("section", None, None, None, None),
        P("section"),
        P(),
        P(None, "mp", None),
        P(),
        P(None, "mp", None, None),
        P(None, "mp", None),
    )
    out_specs = (P(("section", "mp"), "dp"), P(("section", "mp"), "dp"))
    return jax.shard_map(
        on_device, mesh=mesh, in_specs=in_specs, out_specs=out_specs, check_vma=False
    )
```

```python
import math

import jax
import jax.numpy as jnp
from jax import lax
from jax.sharding import PartitionSpec as P

D = 2432
LAT = 64


norm_eps = 1e-06
ema_decay = 0.99
step_size = 0.05


def xor_pairs(n, d, base=0):
    return [(base + i, base + (i ^ d)) for i in range(n)]


def swap(x, axis, n, d, base=0):
    return lax.ppermute(x, axis, xor_pairs(n, d, base))


def gather_in_order(x, axis, n, me, base=0):
    parts = [x] + [swap(x, axis, n, d, base) for d in range(1, n)]
    stacked = jnp.stack(parts)
    return jnp.take(stacked, me ^ jnp.arange(n, dtype=jnp.int32), axis=0)


def relative_blocks(x, axis, n, me):
    width = x.shape[axis] // n
    return jnp.concatenate(
        [lax.dynamic_slice_in_dim(x, (me ^ d) * width, width, axis) for d in range(n)], axis=axis
    )


def gelu_slope(values):
    return jax.vjp(jax.nn.gelu, values)[1](jnp.ones_like(values))[0]


def norm_back(normed, inverse, upstream):
    return inverse * (upstream - normed * jnp.mean(upstream * normed, axis=-1, keepdims=True))


def head_grads(features, w_first, w_second, loss_scale):
    feat_wide = features.astype(jnp.float32)
    inverse = lax.rsqrt(jnp.mean(feat_wide * feat_wide, axis=-1, keepdims=True) + norm_eps)
    normed = feat_wide * inverse
    hidden_pre = jnp.dot(normed.astype(jnp.bfloat16), w_first, preferred_element_type=jnp.float32)
    hidden_act = jax.nn.gelu(hidden_pre).astype(jnp.bfloat16)
    logits = jnp.dot(hidden_act, w_second, preferred_element_type=jnp.float32)
    logit_grad = -loss_scale * jax.nn.sigmoid(-logits)
    act_grad = logit_grad[:, None] * w_second.astype(jnp.float32)[None, :]
    pre_grad = (act_grad * gelu_slope(hidden_pre)).astype(jnp.bfloat16)
    normed_grad = jnp.dot(pre_grad, w_first.T, preferred_element_type=jnp.float32)
    return norm_back(normed, inverse, normed_grad).astype(jnp.bfloat16)


def on_device(
    student_hidden,
    student_weight,
    student_ema,
    noise,
    timesteps,
    patch_embed,
    teacher_weight,
    modulation,
    layer_counts,
    feature_layers,
    head_routes,
    head_owner,
    head_in,
    head_out,
):
    row_count, width = student_hidden.shape
    n_sec = lax.axis_size("section")
    n_mp = lax.axis_size("mp")
    n_dp = lax.axis_size("dp")
    sec = lax.axis_index("section")
    me_dp = lax.axis_index("dp")
    me_mp = lax.axis_index("mp")
    slot_count = teacher_weight.shape[1]
    levels = modulation.shape[2]
    col_width = width // n_dp
    samples = timesteps.shape[0]
    per_sample = row_count // samples

    t_rows = jnp.repeat(timesteps, per_sample)
    noise_level = ((t_rows + 1).astype(jnp.float32) / (levels + 1))[:, None]

    w_cols = gather_in_order(student_weight.astype(jnp.bfloat16), "dp", n_dp, me_dp)
    w_cols = jnp.concatenate(list(w_cols), axis=1)
    row_axes = ("section", "mp")
    row_me = sec * n_mp + me_mp
    w_rows = gather_in_order(w_cols, row_axes, n_sec * n_mp, row_me)
    student_full = w_rows.reshape(width, -1)
    latents = (
        jnp.dot(student_hidden, student_full, preferred_element_type=jnp.float32) * width ** (-0.5)
    ).astype(jnp.bfloat16)
    noisy_input = (
        (1.0 - noise_level) * latents.astype(jnp.float32) + noise_level * noise.astype(jnp.float32)
    ).astype(jnp.bfloat16)
    embed_rel = relative_blocks(patch_embed, 1, n_dp, me_dp)
    start_stream = jnp.dot(noisy_input, embed_rel, preferred_element_type=jnp.float32)

    weights = [
        relative_blocks(
            lax.all_gather(teacher_weight[0, slot_no], "mp", axis=0, tiled=True), 0, n_dp, me_dp
        )
        for slot_no in range(teacher_weight.shape[1])
    ]

    mod_pick = jnp.take(modulation[0], timesteps, axis=1).astype(jnp.float32)
    mod_rows = jnp.repeat(mod_pick, per_sample, axis=1)
    scale_rows = relative_blocks(mod_rows[:, :, 0, :], 2, n_dp, me_dp)
    gate_cols = lax.dynamic_slice_in_dim(mod_rows[:, :, 1, :], me_dp * col_width, col_width, 2)
    active = (jnp.arange(slot_count, dtype=jnp.int32) < layer_counts[0]).astype(jnp.float32)

    saved = []
    taps = []
    stream = start_stream
    for tick in range(n_sec):
        tick_saved = []
        tap = jnp.zeros((row_count, width), jnp.bfloat16)
        for slot_no in range(slot_count):
            inverse = lax.rsqrt(jnp.mean(stream * stream, axis=-1, keepdims=True) + norm_eps)
            normed = stream * inverse
            normed_in = (normed * (1.0 + scale_rows[slot_no])).astype(jnp.bfloat16)
            pre_act = jnp.dot(normed_in, weights[slot_no], preferred_element_type=jnp.float32)
            tick_saved.append((normed, inverse, pre_act))
            part_out = (active[slot_no] * gate_cols[slot_no] * jax.nn.gelu(pre_act)).astype(
                jnp.bfloat16
            )
            joined = [part_out] + [
                swap(part_out, ("section", "dp"), n_dp, d, base=tick * n_dp) for d in range(1, n_dp)
            ]
            joined = jnp.concatenate(joined, axis=1)
            stream = stream + joined.astype(jnp.float32)
            hit = feature_layers[tick] == tick * slot_count + slot_no
            tap = jnp.where(hit, stream.astype(jnp.bfloat16), tap)
        saved.append(tick_saved)
        taps.append(tap)
        if tick + 1 < n_sec:
            sent = lax.ppermute(stream.astype(jnp.bfloat16), "section", [(tick, tick + 1)])
            stream = sent.astype(jnp.float32)

    tap_store = taps[0]
    for tick in range(1, n_sec):
        tap_store = jnp.where(sec == tick, taps[tick], tap_store)
    capacity = 5 * row_count // (4 * n_mp)
    owner_range = jnp.arange(n_mp, dtype=jnp.int32)
    routes = lax.dynamic_index_in_dim(head_routes[:, :, 0], sec, 0, keepdims=False)
    owners_map = lax.dynamic_index_in_dim(head_owner, sec, 0, keepdims=False)
    route_hot = (routes[:, None] == owner_range[None, :]).astype(jnp.int32)
    owner_ids = jnp.sum(route_hot * owners_map[None, :], axis=1)
    owner_hot = (owner_ids[:, None] == owner_range[None, :]).astype(jnp.int32)
    position = jnp.sum(owner_hot * (jnp.cumsum(owner_hot, axis=0) - 1), axis=1)
    target = owner_ids * capacity + position
    dispatch = (
        target[:, None] == jnp.arange(n_mp * capacity, dtype=jnp.int32)[None, :]
    ).astype(jnp.bfloat16)
    send_feat = (
        jnp.dot(dispatch.T, tap_store, preferred_element_type=jnp.float32)
        .astype(jnp.bfloat16)
        .reshape(n_mp, capacity, width)
    )
    items = [lax.dynamic_index_in_dim(send_feat, me_mp, 0, keepdims=False)]
    for d in range(1, n_mp):
        outgoing = lax.dynamic_index_in_dim(send_feat, me_mp ^ d, 0, keepdims=False)
        items.append(swap(outgoing, "mp", n_mp, d))
    loss_scale = width / math.sqrt(row_count * n_mp)
    w_first = relative_blocks(
        lax.dynamic_index_in_dim(head_in[:, 0], sec, 0, keepdims=False), 0, n_dp, me_dp
    )
    w_second = lax.dynamic_index_in_dim(head_out[:, 0], sec, 0, keepdims=False)
    head_result = head_grads(
        jnp.concatenate(items, axis=0), w_first, w_second, loss_scale
    ).reshape(n_mp, capacity, width)
    head_cols = head_result[:, :, :col_width]
    back = [head_cols[0]] + [swap(head_cols[d], "mp", n_mp, d) for d in range(1, n_mp)]
    by_owner = jnp.take(jnp.stack(back), me_mp ^ owner_range, axis=0)
    tap_grads = jnp.dot(
        dispatch, by_owner.reshape(n_mp * capacity, col_width), preferred_element_type=jnp.float32
    )

    my_cols = lambda x: x[..., :col_width]
    grad_stream = jnp.zeros((row_count, col_width), jnp.float32)
    for tick in range(n_sec):
        live = n_sec - 1 - tick
        tick_saved = saved[live]
        for slot_no in reversed(range(slot_count)):
            hit = feature_layers[live] == live * slot_count + slot_no
            grad_stream = grad_stream + jnp.where(hit, tap_grads, 0.0)
            normed, inverse, pre_act = tick_saved[slot_no]
            pre_grad = (
                grad_stream * active[slot_no] * gate_cols[slot_no] * gelu_slope(pre_act)
            ).astype(jnp.bfloat16)
            partial = jnp.dot(
                pre_grad, weights[slot_no].T, preferred_element_type=jnp.float32
            ).astype(jnp.bfloat16)
            partial = lax.optimization_barrier(partial)
            scaled = 1.0 + scale_rows[slot_no]
            row_term = jnp.sum(partial.astype(jnp.float32) * scaled * normed, axis=-1)
            term_hi = row_term.astype(jnp.bfloat16)
            term_lo = (row_term - term_hi.astype(jnp.float32)).astype(jnp.bfloat16)
            terms = jnp.stack([term_hi, term_lo], axis=1)
            pieces = [jnp.concatenate([my_cols(partial), terms], axis=1)]
            for d in range(1, n_dp):
                block = partial[:, d * col_width:(d + 1) * col_width]
                outgoing = jnp.concatenate([block, terms], axis=1)
                pairs = xor_pairs(n_dp, d, live * n_dp)
                pieces.append(lax.ppermute(outgoing, ("section", "dp"), pairs))
            wide = jnp.stack(pieces).astype(jnp.float32)
            input_grad = jnp.zeros((row_count, col_width), jnp.float32)
            row_sum = jnp.zeros((row_count,), jnp.float32)
            for src in range(n_dp):
                input_grad = input_grad + wide[src, :, :col_width]
                row_sum = row_sum + (wide[src, :, col_width] + wide[src, :, col_width + 1])
            row_mean = (row_sum / width)[:, None]
            grad_stream = grad_stream + inverse * (
                input_grad * my_cols(scaled) - my_cols(normed) * row_mean
            )
        if tick + 1 < n_sec:
            sent = lax.ppermute(
                grad_stream.astype(jnp.bfloat16), "section", [(live, live - 1)]
            )
            grad_stream = sent.astype(jnp.float32)

    lat_part = student_weight.shape[1]
    latent_pre = jnp.dot(
        grad_stream.astype(jnp.bfloat16),
        lax.dynamic_slice_in_dim(patch_embed, me_dp * col_width, col_width, 1).T,
        preferred_element_type=jnp.float32,
    )
    got = [lax.dynamic_slice_in_dim(latent_pre, me_dp * lat_part, lat_part, 1)]
    for d in range(1, n_dp):
        block = lax.dynamic_slice_in_dim(latent_pre, (me_dp ^ d) * lat_part, lat_part, 1)
        got.append(lax.ppermute(block, ("section", "dp"), xor_pairs(n_dp, d, 0)))
    got = jnp.take(jnp.stack(got), me_dp ^ jnp.arange(n_dp, dtype=jnp.int32), axis=0)
    lat_sum = got[0]
    for src in range(1, n_dp):
        lat_sum = lat_sum + got[src]
    my_latent = ((1.0 - noise_level) * lat_sum).astype(jnp.bfloat16)
    if n_sec > 1:
        spread = lax.ppermute(my_latent, "section", [(0, s) for s in range(1, n_sec)])
        my_latent = jnp.where(sec == 0, my_latent, spread)

    own_rows = student_weight.shape[0]
    segment_block = width // n_sec
    hidden_cols = lax.dynamic_slice_in_dim(student_hidden, sec * segment_block, segment_block, 1)
    part_grad = lax.dot_general(
        hidden_cols, my_latent, (((0,), (0,)), ((), ())), preferred_element_type=jnp.float32
    ).reshape(n_mp, own_rows, lat_part)
    got = [lax.dynamic_index_in_dim(part_grad, me_mp, 0, keepdims=False)]
    for d in range(1, n_mp):
        outgoing = lax.dynamic_index_in_dim(part_grad, me_mp ^ d, 0, keepdims=False)
        got.append(swap(outgoing, "mp", n_mp, d))
    got = jnp.take(jnp.stack(got), me_mp ^ jnp.arange(n_mp, dtype=jnp.int32), axis=0)
    grad_sum = got[0]
    for src in range(1, n_mp):
        grad_sum = grad_sum + got[src]
    student_grad = grad_sum * width ** (-0.5)

    local_sq = jnp.sum(student_grad * student_grad).reshape(1)
    sq = gather_in_order(local_sq, "section", n_sec, sec).reshape(-1)
    sq = gather_in_order(sq, "dp", n_dp, me_dp).reshape(-1)
    sq = gather_in_order(sq, "mp", n_mp, me_mp).reshape(-1)
    total_sq = jnp.sum(sq)
    mean_square = total_sq / (width * LAT)
    student_update = student_grad * lax.rsqrt(mean_square + norm_eps)
    ema_new = ema_decay * student_ema + (1.0 - ema_decay) * (
        student_weight - step_size * student_update
    )
    return (student_update, ema_new)


def solution(mesh):
    in_specs = (
        P("mp", None),
        P(("section", "mp"), "dp"),
        P(("section", "mp"), "dp"),
        P("mp", None),
        P("mp"),
        P(),
        P("section", None, "mp", "dp"),
        P("section", None, None, None, None),
        P("section"),
        P(),
        P(None, "mp", None),
        P(),
        P(None, "mp", None, None),
        P(None, "mp", None),
    )
    out_specs = (P(("section", "mp"), "dp"), P(("section", "mp"), "dp"))
    return jax.shard_map(
        on_device, mesh=mesh, in_specs=in_specs, out_specs=out_specs, check_vma=False
    )
```

```python
import math

import jax
import jax.numpy as jnp
from jax import lax
from jax.sharding import PartitionSpec as P

D = 2432
LAT = 64


norm_eps = 1e-06
ema_decay = 0.99
step_size = 0.05


def xor_pairs(n, d, base=0):
    return [(base + i, base + (i ^ d)) for i in range(n)]


def swap(x, axis, n, d, base=0):
    return lax.ppermute(x, axis, xor_pairs(n, d, base))


def gather_in_order(x, axis, n, me, base=0):
    parts = [x] + [swap(x, axis, n, d, base) for d in range(1, n)]
    stacked = jnp.stack(parts)
    return jnp.take(stacked, me ^ jnp.arange(n, dtype=jnp.int32), axis=0)


def relative_blocks(x, axis, n, me):
    width = x.shape[axis] // n
    return jnp.concatenate(
        [lax.dynamic_slice_in_dim(x, (me ^ d) * width, width, axis) for d in range(n)], axis=axis
    )


def gelu_slope(values):
    return jax.vjp(jax.nn.gelu, values)[1](jnp.ones_like(values))[0]


def norm_back(normed, inverse, upstream):
    return inverse * (upstream - normed * jnp.mean(upstream * normed, axis=-1, keepdims=True))


def head_grads(features, w_first, w_second, loss_scale):
    feat_wide = features.astype(jnp.float32)
    inverse = lax.rsqrt(jnp.mean(feat_wide * feat_wide, axis=-1, keepdims=True) + norm_eps)
    normed = feat_wide * inverse
    hidden_pre = jnp.dot(normed.astype(jnp.bfloat16), w_first, preferred_element_type=jnp.float32)
    hidden_act = jax.nn.gelu(hidden_pre).astype(jnp.bfloat16)
    logits = jnp.dot(hidden_act, w_second, preferred_element_type=jnp.float32)
    logit_grad = -loss_scale * jax.nn.sigmoid(-logits)
    act_grad = logit_grad[:, None] * w_second.astype(jnp.float32)[None, :]
    pre_grad = (act_grad * gelu_slope(hidden_pre)).astype(jnp.bfloat16)
    normed_grad = jnp.dot(pre_grad, w_first.T, preferred_element_type=jnp.float32)
    return norm_back(normed, inverse, normed_grad).astype(jnp.bfloat16)


def on_device(
    student_hidden,
    student_weight,
    student_ema,
    noise,
    timesteps,
    patch_embed,
    teacher_weight,
    modulation,
    layer_counts,
    feature_layers,
    head_routes,
    head_owner,
    head_in,
    head_out,
):
    row_count, width = student_hidden.shape
    n_sec = lax.axis_size("section")
    n_mp = lax.axis_size("mp")
    n_dp = lax.axis_size("dp")
    sec = lax.axis_index("section")
    me_dp = lax.axis_index("dp")
    me_mp = lax.axis_index("mp")
    slot_count = teacher_weight.shape[1]
    levels = modulation.shape[2]
    col_width = width // n_dp
    samples = timesteps.shape[0]
    per_sample = row_count // samples

    t_rows = jnp.repeat(timesteps, per_sample)
    noise_level = ((t_rows + 1).astype(jnp.float32) / (levels + 1))[:, None]

    w_cols = gather_in_order(student_weight.astype(jnp.bfloat16), "dp", n_dp, me_dp)
    w_cols = jnp.concatenate(list(w_cols), axis=1)
    row_axes = ("section", "mp")
    row_me = sec * n_mp + me_mp
    w_rows = gather_in_order(w_cols, row_axes, n_sec * n_mp, row_me)
    student_full = w_rows.reshape(width, -1)
    latents = (
        jnp.dot(student_hidden, student_full, preferred_element_type=jnp.float32) * width ** (-0.5)
    ).astype(jnp.bfloat16)
    noisy_input = (
        (1.0 - noise_level) * latents.astype(jnp.float32) + noise_level * noise.astype(jnp.float32)
    ).astype(jnp.bfloat16)
    embed_rel = relative_blocks(patch_embed, 1, n_dp, me_dp)
    start_stream = jnp.dot(noisy_input, embed_rel, preferred_element_type=jnp.float32)

    def gather_set(local, role):
        pieces, arrived = [], []
        for slot_no in range(local.shape[0]):
            parts = [local[slot_no]]
            for d in range(1, n_mp):
                got = lax.ppermute(
                    local[slot_no], ("section", "mp"), xor_pairs(n_mp, d, role * n_mp)
                )
                parts.append(got)
                arrived.append(got[0, 0].astype(jnp.float32))
            rows = jnp.take(jnp.stack(parts), me_mp ^ jnp.arange(n_mp, dtype=jnp.int32), axis=0)
            pieces.append(relative_blocks(rows.reshape(width, -1), 0, n_dp, me_dp))
        return pieces, sum(arrived)

    weight_sets = []
    local_weights = teacher_weight[0]
    for role in range(n_sec):
        pieces, token = gather_set(local_weights, role)
        weight_sets.append(pieces)
        if role + 1 < n_sec:
            passed = lax.ppermute(token, "section", [(role, role + 1)])
            local_weights, _ = lax.optimization_barrier((teacher_weight[0], passed))

    mod_pick = jnp.take(modulation[0], timesteps, axis=1).astype(jnp.float32)
    mod_rows = jnp.repeat(mod_pick, per_sample, axis=1)
    scale_rows = relative_blocks(mod_rows[:, :, 0, :], 2, n_dp, me_dp)
    gate_cols = lax.dynamic_slice_in_dim(mod_rows[:, :, 1, :], me_dp * col_width, col_width, 2)
    active = (jnp.arange(slot_count, dtype=jnp.int32) < layer_counts[0]).astype(jnp.float32)

    saved = []
    taps = []
    stream = start_stream
    for tick in range(n_sec):
        tick_saved = []
        tap = jnp.zeros((row_count, width), jnp.bfloat16)
        for slot_no in range(slot_count):
            inverse = lax.rsqrt(jnp.mean(stream * stream, axis=-1, keepdims=True) + norm_eps)
            normed = stream * inverse
            normed_in = (normed * (1.0 + scale_rows[slot_no])).astype(jnp.bfloat16)
            pre_act = jnp.dot(
                normed_in, weight_sets[tick][slot_no], preferred_element_type=jnp.float32
            )
            tick_saved.append((normed, inverse, pre_act))
            part_out = (active[slot_no] * gate_cols[slot_no] * jax.nn.gelu(pre_act)).astype(
                jnp.bfloat16
            )
            joined = [part_out] + [
                swap(part_out, ("section", "dp"), n_dp, d, base=tick * n_dp) for d in range(1, n_dp)
            ]
            joined = jnp.concatenate(joined, axis=1)
            stream = stream + joined.astype(jnp.float32)
            hit = feature_layers[tick] == tick * slot_count + slot_no
            tap = jnp.where(hit, stream.astype(jnp.bfloat16), tap)
        saved.append(tick_saved)
        taps.append(tap)
        if tick + 1 < n_sec:
            sent = lax.ppermute(stream.astype(jnp.bfloat16), "section", [(tick, tick + 1)])
            stream = sent.astype(jnp.float32)

    tap_store = taps[0]
    for tick in range(1, n_sec):
        tap_store = jnp.where(sec == tick, taps[tick], tap_store)
    capacity = 5 * row_count // (4 * n_mp)
    owner_range = jnp.arange(n_mp, dtype=jnp.int32)
    routes = lax.dynamic_index_in_dim(head_routes[:, :, 0], sec, 0, keepdims=False)
    owners_map = lax.dynamic_index_in_dim(head_owner, sec, 0, keepdims=False)
    route_hot = (routes[:, None] == owner_range[None, :]).astype(jnp.int32)
    owner_ids = jnp.sum(route_hot * owners_map[None, :], axis=1)
    owner_hot = (owner_ids[:, None] == owner_range[None, :]).astype(jnp.int32)
    position = jnp.sum(owner_hot * (jnp.cumsum(owner_hot, axis=0) - 1), axis=1)
    target = owner_ids * capacity + position
    dispatch = (
        target[:, None] == jnp.arange(n_mp * capacity, dtype=jnp.int32)[None, :]
    ).astype(jnp.bfloat16)
    send_feat = (
        jnp.dot(dispatch.T, tap_store, preferred_element_type=jnp.float32)
        .astype(jnp.bfloat16)
        .reshape(n_mp, capacity, width)
    )
    items = [lax.dynamic_index_in_dim(send_feat, me_mp, 0, keepdims=False)]
    for d in range(1, n_mp):
        outgoing = lax.dynamic_index_in_dim(send_feat, me_mp ^ d, 0, keepdims=False)
        items.append(swap(outgoing, "mp", n_mp, d))
    loss_scale = width / math.sqrt(row_count * n_mp)
    w_first = relative_blocks(
        lax.dynamic_index_in_dim(head_in[:, 0], sec, 0, keepdims=False), 0, n_dp, me_dp
    )
    w_second = lax.dynamic_index_in_dim(head_out[:, 0], sec, 0, keepdims=False)
    head_result = head_grads(
        jnp.concatenate(items, axis=0), w_first, w_second, loss_scale
    ).reshape(n_mp, capacity, width)
    head_cols = head_result[:, :, :col_width]
    back = [head_cols[0]] + [swap(head_cols[d], "mp", n_mp, d) for d in range(1, n_mp)]
    by_owner = jnp.take(jnp.stack(back), me_mp ^ owner_range, axis=0)
    tap_grads = jnp.dot(
        dispatch, by_owner.reshape(n_mp * capacity, col_width), preferred_element_type=jnp.float32
    )

    my_cols = lambda x: x[..., :col_width]
    grad_stream = jnp.zeros((row_count, col_width), jnp.float32)
    for tick in range(n_sec):
        live = n_sec - 1 - tick
        tick_saved = saved[live]
        for slot_no in reversed(range(slot_count)):
            hit = feature_layers[live] == live * slot_count + slot_no
            grad_stream = grad_stream + jnp.where(hit, tap_grads, 0.0)
            normed, inverse, pre_act = tick_saved[slot_no]
            pre_grad = (
                grad_stream * active[slot_no] * gate_cols[slot_no] * gelu_slope(pre_act)
            ).astype(jnp.bfloat16)
            partial = jnp.dot(
                pre_grad, weight_sets[live][slot_no].T, preferred_element_type=jnp.float32
            ).astype(jnp.bfloat16)
            partial = lax.optimization_barrier(partial)
            scaled = 1.0 + scale_rows[slot_no]
            row_term = jnp.sum(partial.astype(jnp.float32) * scaled * normed, axis=-1)
            term_hi = row_term.astype(jnp.bfloat16)
            term_lo = (row_term - term_hi.astype(jnp.float32)).astype(jnp.bfloat16)
            terms = jnp.stack([term_hi, term_lo], axis=1)
            pieces = [jnp.concatenate([my_cols(partial), terms], axis=1)]
            for d in range(1, n_dp):
                block = partial[:, d * col_width:(d + 1) * col_width]
                outgoing = jnp.concatenate([block, terms], axis=1)
                pairs = xor_pairs(n_dp, d, live * n_dp)
                pieces.append(lax.ppermute(outgoing, ("section", "dp"), pairs))
            wide = jnp.stack(pieces).astype(jnp.float32)
            input_grad = jnp.zeros((row_count, col_width), jnp.float32)
            row_sum = jnp.zeros((row_count,), jnp.float32)
            for src in range(n_dp):
                input_grad = input_grad + wide[src, :, :col_width]
                row_sum = row_sum + (wide[src, :, col_width] + wide[src, :, col_width + 1])
            row_mean = (row_sum / width)[:, None]
            grad_stream = grad_stream + inverse * (
                input_grad * my_cols(scaled) - my_cols(normed) * row_mean
            )
        if tick + 1 < n_sec:
            sent = lax.ppermute(
                grad_stream.astype(jnp.bfloat16), "section", [(live, live - 1)]
            )
            grad_stream = sent.astype(jnp.float32)

    lat_part = student_weight.shape[1]
    latent_pre = jnp.dot(
        grad_stream.astype(jnp.bfloat16),
        lax.dynamic_slice_in_dim(patch_embed, me_dp * col_width, col_width, 1).T,
        preferred_element_type=jnp.float32,
    )
    got = [lax.dynamic_slice_in_dim(latent_pre, me_dp * lat_part, lat_part, 1)]
    for d in range(1, n_dp):
        block = lax.dynamic_slice_in_dim(latent_pre, (me_dp ^ d) * lat_part, lat_part, 1)
        got.append(lax.ppermute(block, ("section", "dp"), xor_pairs(n_dp, d, 0)))
    got = jnp.take(jnp.stack(got), me_dp ^ jnp.arange(n_dp, dtype=jnp.int32), axis=0)
    lat_sum = got[0]
    for src in range(1, n_dp):
        lat_sum = lat_sum + got[src]
    my_latent = ((1.0 - noise_level) * lat_sum).astype(jnp.bfloat16)
    if n_sec > 1:
        spread = lax.ppermute(my_latent, "section", [(0, s) for s in range(1, n_sec)])
        my_latent = jnp.where(sec == 0, my_latent, spread)

    own_rows = student_weight.shape[0]
    segment_block = width // n_sec
    hidden_cols = lax.dynamic_slice_in_dim(student_hidden, sec * segment_block, segment_block, 1)
    part_grad = lax.dot_general(
        hidden_cols, my_latent, (((0,), (0,)), ((), ())), preferred_element_type=jnp.float32
    ).reshape(n_mp, own_rows, lat_part)
    got = [lax.dynamic_index_in_dim(part_grad, me_mp, 0, keepdims=False)]
    for d in range(1, n_mp):
        outgoing = lax.dynamic_index_in_dim(part_grad, me_mp ^ d, 0, keepdims=False)
        got.append(swap(outgoing, "mp", n_mp, d))
    got = jnp.take(jnp.stack(got), me_mp ^ jnp.arange(n_mp, dtype=jnp.int32), axis=0)
    grad_sum = got[0]
    for src in range(1, n_mp):
        grad_sum = grad_sum + got[src]
    student_grad = grad_sum * width ** (-0.5)

    local_sq = jnp.sum(student_grad * student_grad).reshape(1)
    sq = gather_in_order(local_sq, "section", n_sec, sec).reshape(-1)
    sq = gather_in_order(sq, "dp", n_dp, me_dp).reshape(-1)
    sq = gather_in_order(sq, "mp", n_mp, me_mp).reshape(-1)
    total_sq = jnp.sum(sq)
    mean_square = total_sq / (width * LAT)
    student_update = student_grad * lax.rsqrt(mean_square + norm_eps)
    ema_new = ema_decay * student_ema + (1.0 - ema_decay) * (
        student_weight - step_size * student_update
    )
    return (student_update, ema_new)


def solution(mesh):
    in_specs = (
        P("mp", None),
        P(("section", "mp"), "dp"),
        P(("section", "mp"), "dp"),
        P("mp", None),
        P("mp"),
        P(),
        P("section", None, "mp", "dp"),
        P("section", None, None, None, None),
        P("section"),
        P(),
        P(None, "mp", None),
        P(),
        P(None, "mp", None, None),
        P(None, "mp", None),
    )
    out_specs = (P(("section", "mp"), "dp"), P(("section", "mp"), "dp"))
    return jax.shard_map(
        on_device, mesh=mesh, in_specs=in_specs, out_specs=out_specs, check_vma=False
    )
```

```python
import math

import jax
import jax.numpy as jnp
from jax import lax
from jax.sharding import PartitionSpec as P

D = 2432
LAT = 64


norm_eps = 1e-06
ema_decay = 0.99
step_size = 0.05


def xor_pairs(n, d, base=0):
    return [(base + i, base + (i ^ d)) for i in range(n)]


def swap(x, axis, n, d, base=0):
    return lax.ppermute(x, axis, xor_pairs(n, d, base))


def gather_in_order(x, axis, n, me, base=0):
    parts = [x] + [swap(x, axis, n, d, base) for d in range(1, n)]
    stacked = jnp.stack(parts)
    return jnp.take(stacked, me ^ jnp.arange(n, dtype=jnp.int32), axis=0)


def relative_blocks(x, axis, n, me):
    width = x.shape[axis] // n
    return jnp.concatenate(
        [lax.dynamic_slice_in_dim(x, (me ^ d) * width, width, axis) for d in range(n)], axis=axis
    )


def gelu_slope(values):
    return jax.vjp(jax.nn.gelu, values)[1](jnp.ones_like(values))[0]


def norm_back(normed, inverse, upstream):
    return inverse * (upstream - normed * jnp.mean(upstream * normed, axis=-1, keepdims=True))


def head_grads(features, w_first, w_second, loss_scale):
    feat_wide = features.astype(jnp.float32)
    inverse = lax.rsqrt(jnp.mean(feat_wide * feat_wide, axis=-1, keepdims=True) + norm_eps)
    normed = feat_wide * inverse
    hidden_pre = jnp.dot(normed.astype(jnp.bfloat16), w_first, preferred_element_type=jnp.float32)
    hidden_act = jax.nn.gelu(hidden_pre).astype(jnp.bfloat16)
    logits = jnp.dot(hidden_act, w_second, preferred_element_type=jnp.float32)
    logit_grad = -loss_scale * jax.nn.sigmoid(-logits)
    act_grad = logit_grad[:, None] * w_second.astype(jnp.float32)[None, :]
    pre_grad = (act_grad * gelu_slope(hidden_pre)).astype(jnp.bfloat16)
    normed_grad = jnp.dot(pre_grad, w_first.T, preferred_element_type=jnp.float32)
    return norm_back(normed, inverse, normed_grad).astype(jnp.bfloat16)


def on_device(
    student_hidden,
    student_weight,
    student_ema,
    noise,
    timesteps,
    patch_embed,
    teacher_weight,
    modulation,
    layer_counts,
    feature_layers,
    head_routes,
    head_owner,
    head_in,
    head_out,
):
    row_count, width = student_hidden.shape
    n_sec = lax.axis_size("section")
    n_mp = lax.axis_size("mp")
    n_dp = lax.axis_size("dp")
    sec = lax.axis_index("section")
    me_dp = lax.axis_index("dp")
    me_mp = lax.axis_index("mp")
    slot_count = teacher_weight.shape[1]
    levels = modulation.shape[2]
    col_width = width // n_dp
    samples = timesteps.shape[0]
    per_sample = row_count // samples

    t_rows = jnp.repeat(timesteps, per_sample)
    noise_level = ((t_rows + 1).astype(jnp.float32) / (levels + 1))[:, None]

    w_cols = gather_in_order(student_weight.astype(jnp.bfloat16), "dp", n_dp, me_dp)
    w_cols = jnp.concatenate(list(w_cols), axis=1)
    row_axes = ("section", "mp")
    row_me = sec * n_mp + me_mp
    w_rows = gather_in_order(w_cols, row_axes, n_sec * n_mp, row_me)
    student_full = w_rows.reshape(width, -1)
    latents = (
        jnp.dot(student_hidden, student_full, preferred_element_type=jnp.float32) * width ** (-0.5)
    ).astype(jnp.bfloat16)
    noisy_input = (
        (1.0 - noise_level) * latents.astype(jnp.float32) + noise_level * noise.astype(jnp.float32)
    ).astype(jnp.bfloat16)
    embed_rel = relative_blocks(patch_embed, 1, n_dp, me_dp)
    start_stream = jnp.dot(noisy_input, embed_rel, preferred_element_type=jnp.float32)

    weights = [
        relative_blocks(
            lax.all_gather(teacher_weight[0, slot_no], "mp", axis=0, tiled=True), 0, n_dp, me_dp
        )
        for slot_no in range(teacher_weight.shape[1])
    ]

    mod_pick = jnp.take(modulation[0], timesteps, axis=1).astype(jnp.float32)
    mod_rows = jnp.repeat(mod_pick, per_sample, axis=1)
    scale_rows = relative_blocks(mod_rows[:, :, 0, :], 2, n_dp, me_dp)
    gate_cols = lax.dynamic_slice_in_dim(mod_rows[:, :, 1, :], me_dp * col_width, col_width, 2)
    active = (jnp.arange(slot_count, dtype=jnp.int32) < layer_counts[0]).astype(jnp.float32)

    saved = []
    taps = []
    stream = start_stream
    for tick in range(n_sec):
        tick_saved = []
        tap = jnp.zeros((row_count, width), jnp.bfloat16)
        for slot_no in range(slot_count):
            inverse = lax.rsqrt(jnp.mean(stream * stream, axis=-1, keepdims=True) + norm_eps)
            normed = stream * inverse
            normed_in = (normed * (1.0 + scale_rows[slot_no])).astype(jnp.bfloat16)
            pre_act = jnp.dot(normed_in, weights[slot_no], preferred_element_type=jnp.float32)
            tick_saved.append((normed, inverse, pre_act))
            part_out = (active[slot_no] * gate_cols[slot_no] * jax.nn.gelu(pre_act)).astype(
                jnp.bfloat16
            )
            joined = [part_out] + [
                swap(part_out, ("section", "dp"), n_dp, d, base=tick * n_dp) for d in range(1, n_dp)
            ]
            joined = jnp.concatenate(joined, axis=1)
            stream = stream + joined.astype(jnp.float32)
            hit = feature_layers[tick] == tick * slot_count + slot_no
            tap = jnp.where(hit, stream.astype(jnp.bfloat16), tap)
        saved.append(tick_saved)
        taps.append(tap)
        if tick + 1 < n_sec:
            sent = lax.ppermute(stream.astype(jnp.bfloat16), "section", [(tick, tick + 1)])
            stream = sent.astype(jnp.float32)

    tap_store = taps[0]
    for tick in range(1, n_sec):
        tap_store = jnp.where(sec == tick, taps[tick], tap_store)
    capacity = 5 * row_count // (4 * n_mp)
    owner_range = jnp.arange(n_mp, dtype=jnp.int32)
    routes = lax.dynamic_index_in_dim(head_routes[:, :, 0], sec, 0, keepdims=False)
    owners_map = lax.dynamic_index_in_dim(head_owner, sec, 0, keepdims=False)
    route_hot = (routes[:, None] == owner_range[None, :]).astype(jnp.int32)
    owner_ids = jnp.sum(route_hot * owners_map[None, :], axis=1)
    owner_hot = (owner_ids[:, None] == owner_range[None, :]).astype(jnp.int32)
    position = jnp.sum(owner_hot * (jnp.cumsum(owner_hot, axis=0) - 1), axis=1)
    target = owner_ids * capacity + position
    dispatch = (
        target[:, None] == jnp.arange(n_mp * capacity, dtype=jnp.int32)[None, :]
    ).astype(jnp.bfloat16)
    send_feat = (
        jnp.dot(dispatch.T, tap_store, preferred_element_type=jnp.float32)
        .astype(jnp.bfloat16)
        .reshape(n_mp, capacity, width)
    )
    items = [lax.dynamic_index_in_dim(send_feat, me_mp, 0, keepdims=False)]
    for d in range(1, n_mp):
        outgoing = lax.dynamic_index_in_dim(send_feat, me_mp ^ d, 0, keepdims=False)
        items.append(swap(outgoing, "mp", n_mp, d))
    loss_scale = width / math.sqrt(row_count * n_mp)
    w_first = relative_blocks(
        lax.dynamic_index_in_dim(head_in[:, 0], sec, 0, keepdims=False), 0, n_dp, me_dp
    )
    w_second = lax.dynamic_index_in_dim(head_out[:, 0], sec, 0, keepdims=False)
    head_result = head_grads(
        jnp.concatenate(items, axis=0), w_first, w_second, loss_scale
    ).reshape(n_mp, capacity, width)
    head_cols = head_result[:, :, :col_width]
    back = [head_cols[0]] + [swap(head_cols[d], "mp", n_mp, d) for d in range(1, n_mp)]
    by_owner = jnp.take(jnp.stack(back), me_mp ^ owner_range, axis=0)
    tap_grads = jnp.dot(
        dispatch, by_owner.reshape(n_mp * capacity, col_width), preferred_element_type=jnp.float32
    )

    my_cols = lambda x: x[..., :col_width]
    grad_stream = jnp.zeros((row_count, col_width), jnp.float32)
    for tick in range(n_sec):
        live = n_sec - 1 - tick
        tick_saved = saved[live]
        for slot_no in reversed(range(slot_count)):
            hit = feature_layers[live] == live * slot_count + slot_no
            grad_stream = grad_stream + jnp.where(hit, tap_grads, 0.0)
            normed, inverse, pre_act = tick_saved[slot_no]
            pre_grad = (
                grad_stream * active[slot_no] * gate_cols[slot_no] * gelu_slope(pre_act)
            ).astype(jnp.bfloat16)
            partial = jnp.dot(
                pre_grad, weights[slot_no].T, preferred_element_type=jnp.float32
            ).astype(jnp.bfloat16)
            partial = lax.optimization_barrier(partial)
            scaled = 1.0 + scale_rows[slot_no]
            row_term = jnp.sum(partial.astype(jnp.float32) * scaled * normed, axis=-1)
            pieces = [my_cols(partial)]
            terms = [row_term[None, :]]
            for d in range(1, n_dp):
                block = partial[:, d * col_width:(d + 1) * col_width]
                pairs = xor_pairs(n_dp, d, live * n_dp)
                pieces.append(lax.ppermute(block, ("section", "dp"), pairs))
                terms.append(lax.ppermute(row_term[None, :], ("section", "dp"), pairs))
            input_grad = jnp.zeros((row_count, col_width), jnp.float32)
            row_sum = jnp.zeros((row_count,), jnp.float32)
            for src in range(n_dp):
                input_grad = input_grad + pieces[src].astype(jnp.float32)
                row_sum = row_sum + terms[src][0]
            row_mean = (row_sum / width)[:, None]
            grad_stream = grad_stream + inverse * (
                input_grad * my_cols(scaled) - my_cols(normed) * row_mean
            )
        if tick + 1 < n_sec:
            sent = lax.ppermute(
                grad_stream.astype(jnp.bfloat16), "section", [(live, live - 1)]
            )
            grad_stream = sent.astype(jnp.float32)

    lat_part = student_weight.shape[1]
    latent_pre = jnp.dot(
        grad_stream.astype(jnp.bfloat16),
        lax.dynamic_slice_in_dim(patch_embed, me_dp * col_width, col_width, 1).T,
        preferred_element_type=jnp.float32,
    )
    got = [lax.dynamic_slice_in_dim(latent_pre, me_dp * lat_part, lat_part, 1)]
    for d in range(1, n_dp):
        block = lax.dynamic_slice_in_dim(latent_pre, (me_dp ^ d) * lat_part, lat_part, 1)
        got.append(lax.ppermute(block, ("section", "dp"), xor_pairs(n_dp, d, 0)))
    got = jnp.take(jnp.stack(got), me_dp ^ jnp.arange(n_dp, dtype=jnp.int32), axis=0)
    lat_sum = got[0]
    for src in range(1, n_dp):
        lat_sum = lat_sum + got[src]
    my_latent = ((1.0 - noise_level) * lat_sum).astype(jnp.bfloat16)
    if n_sec > 1:
        spread = lax.ppermute(my_latent, "section", [(0, s) for s in range(1, n_sec)])
        my_latent = jnp.where(sec == 0, my_latent, spread)

    own_rows = student_weight.shape[0]
    segment_block = width // n_sec
    hidden_cols = lax.dynamic_slice_in_dim(student_hidden, sec * segment_block, segment_block, 1)
    part_grad = lax.dot_general(
        hidden_cols, my_latent, (((0,), (0,)), ((), ())), preferred_element_type=jnp.float32
    ).reshape(n_mp, own_rows, lat_part)
    got = [lax.dynamic_index_in_dim(part_grad, me_mp, 0, keepdims=False)]
    for d in range(1, n_mp):
        outgoing = lax.dynamic_index_in_dim(part_grad, me_mp ^ d, 0, keepdims=False)
        got.append(swap(outgoing, "mp", n_mp, d))
    got = jnp.take(jnp.stack(got), me_mp ^ jnp.arange(n_mp, dtype=jnp.int32), axis=0)
    grad_sum = got[0]
    for src in range(1, n_mp):
        grad_sum = grad_sum + got[src]
    student_grad = grad_sum * width ** (-0.5)

    local_sq = jnp.sum(student_grad * student_grad).reshape(1)
    sq = gather_in_order(local_sq, "section", n_sec, sec).reshape(-1)
    sq = gather_in_order(sq, "dp", n_dp, me_dp).reshape(-1)
    sq = gather_in_order(sq, "mp", n_mp, me_mp).reshape(-1)
    total_sq = jnp.sum(sq)
    mean_square = total_sq / (width * LAT)
    student_update = student_grad * lax.rsqrt(mean_square + norm_eps)
    ema_new = ema_decay * student_ema + (1.0 - ema_decay) * (
        student_weight - step_size * student_update
    )
    return (student_update, ema_new)


def solution(mesh):
    in_specs = (
        P("mp", None),
        P(("section", "mp"), "dp"),
        P(("section", "mp"), "dp"),
        P("mp", None),
        P("mp"),
        P(),
        P("section", None, "mp", "dp"),
        P("section", None, None, None, None),
        P("section"),
        P(),
        P(None, "mp", None),
        P(),
        P(None, "mp", None, None),
        P(None, "mp", None),
    )
    out_specs = (P(("section", "mp"), "dp"), P(("section", "mp"), "dp"))
    return jax.shard_map(
        on_device, mesh=mesh, in_specs=in_specs, out_specs=out_specs, check_vma=False
    )
```

```python
import math

import jax
import jax.numpy as jnp
from jax import lax
from jax.sharding import PartitionSpec as P

D = 2432
LAT = 64


norm_eps = 1e-06
ema_decay = 0.99
step_size = 0.05


def xor_pairs(n, d, base=0):
    return [(base + i, base + (i ^ d)) for i in range(n)]


def swap(x, axis, n, d, base=0):
    return lax.ppermute(x, axis, xor_pairs(n, d, base))


def gather_in_order(x, axis, n, me, base=0):
    parts = [x] + [swap(x, axis, n, d, base) for d in range(1, n)]
    stacked = jnp.stack(parts)
    return jnp.take(stacked, me ^ jnp.arange(n, dtype=jnp.int32), axis=0)


def relative_blocks(x, axis, n, me):
    width = x.shape[axis] // n
    return jnp.concatenate(
        [lax.dynamic_slice_in_dim(x, (me ^ d) * width, width, axis) for d in range(n)], axis=axis
    )


def gelu_slope(values):
    return jax.vjp(jax.nn.gelu, values)[1](jnp.ones_like(values))[0]


def norm_back(normed, inverse, upstream):
    return inverse * (upstream - normed * jnp.mean(upstream * normed, axis=-1, keepdims=True))


def head_grads(features, w_first, w_second, loss_scale):
    feat_wide = features.astype(jnp.float32)
    inverse = lax.rsqrt(jnp.mean(feat_wide * feat_wide, axis=-1, keepdims=True) + norm_eps)
    normed = feat_wide * inverse
    hidden_pre = jnp.dot(normed.astype(jnp.bfloat16), w_first, preferred_element_type=jnp.float32)
    hidden_act = jax.nn.gelu(hidden_pre).astype(jnp.bfloat16)
    logits = jnp.dot(hidden_act, w_second, preferred_element_type=jnp.float32)
    logit_grad = -loss_scale * jax.nn.sigmoid(-logits)
    act_grad = logit_grad[:, None] * w_second.astype(jnp.float32)[None, :]
    pre_grad = (act_grad * gelu_slope(hidden_pre)).astype(jnp.bfloat16)
    normed_grad = jnp.dot(pre_grad, w_first.T, preferred_element_type=jnp.float32)
    return norm_back(normed, inverse, normed_grad).astype(jnp.bfloat16)


def on_device(
    student_hidden,
    student_weight,
    student_ema,
    noise,
    timesteps,
    patch_embed,
    teacher_weight,
    modulation,
    layer_counts,
    feature_layers,
    head_routes,
    head_owner,
    head_in,
    head_out,
):
    row_count, width = student_hidden.shape
    n_sec = lax.axis_size("section")
    n_mp = lax.axis_size("mp")
    n_dp = lax.axis_size("dp")
    sec = lax.axis_index("section")
    me_dp = lax.axis_index("dp")
    me_mp = lax.axis_index("mp")
    slot_count = teacher_weight.shape[1]
    levels = modulation.shape[2]
    col_width = width // n_dp
    samples = timesteps.shape[0]
    per_sample = row_count // samples

    t_rows = jnp.repeat(timesteps, per_sample)
    noise_level = ((t_rows + 1).astype(jnp.float32) / (levels + 1))[:, None]

    w_cols = gather_in_order(student_weight.astype(jnp.bfloat16), "dp", n_dp, me_dp)
    w_cols = jnp.concatenate(list(w_cols), axis=1)
    row_axes = ("section", "mp")
    row_me = sec * n_mp + me_mp
    w_rows = gather_in_order(w_cols, row_axes, n_sec * n_mp, row_me)
    student_full = w_rows.reshape(width, -1)
    latents = (
        jnp.dot(student_hidden, student_full, preferred_element_type=jnp.float32) * width ** (-0.5)
    ).astype(jnp.bfloat16)
    noisy_input = (
        (1.0 - noise_level) * latents.astype(jnp.float32) + noise_level * noise.astype(jnp.float32)
    ).astype(jnp.bfloat16)
    embed_rel = relative_blocks(patch_embed, 1, n_dp, me_dp)
    start_stream = jnp.dot(noisy_input, embed_rel, preferred_element_type=jnp.float32)

    weights = [
        relative_blocks(
            lax.all_gather(teacher_weight[0, slot_no], "mp", axis=0, tiled=True), 0, n_dp, me_dp
        )
        for slot_no in range(teacher_weight.shape[1])
    ]

    mod_pick = jnp.take(modulation[0], timesteps, axis=1).astype(jnp.float32)
    mod_rows = jnp.repeat(mod_pick, per_sample, axis=1)
    scale_rows = relative_blocks(mod_rows[:, :, 0, :], 2, n_dp, me_dp)
    gate_cols = lax.dynamic_slice_in_dim(mod_rows[:, :, 1, :], me_dp * col_width, col_width, 2)
    active = (jnp.arange(slot_count, dtype=jnp.int32) < layer_counts[0]).astype(jnp.float32)

    saved = []
    taps = []
    stream = start_stream
    for tick in range(n_sec):
        tick_saved = []
        tap = jnp.zeros((row_count, width), jnp.bfloat16)
        for slot_no in range(slot_count):
            inverse = lax.rsqrt(jnp.mean(stream * stream, axis=-1, keepdims=True) + norm_eps)
            normed = stream * inverse
            normed_in = (normed * (1.0 + scale_rows[slot_no])).astype(jnp.bfloat16)
            pre_act = jnp.dot(normed_in, weights[slot_no], preferred_element_type=jnp.float32)
            tick_saved.append((normed, inverse, pre_act))
            part_out = (active[slot_no] * gate_cols[slot_no] * jax.nn.gelu(pre_act)).astype(
                jnp.bfloat16
            )
            joined = [part_out] + [
                swap(part_out, ("section", "dp"), n_dp, d, base=tick * n_dp) for d in range(1, n_dp)
            ]
            joined = jnp.concatenate(joined, axis=1)
            stream = stream + joined.astype(jnp.float32)
            hit = feature_layers[tick] == tick * slot_count + slot_no
            tap = jnp.where(hit, stream.astype(jnp.bfloat16), tap)
        saved.append(tick_saved)
        taps.append(tap)
        if tick + 1 < n_sec:
            sent = lax.ppermute(stream.astype(jnp.bfloat16), "section", [(tick, tick + 1)])
            stream = sent.astype(jnp.float32)

    tap_store = taps[0]
    for tick in range(1, n_sec):
        tap_store = jnp.where(sec == tick, taps[tick], tap_store)
    capacity = 5 * row_count // (4 * n_mp)
    owner_range = jnp.arange(n_mp, dtype=jnp.int32)
    routes = lax.dynamic_index_in_dim(head_routes[:, :, 0], sec, 0, keepdims=False)
    owners_map = lax.dynamic_index_in_dim(head_owner, sec, 0, keepdims=False)
    route_hot = (routes[:, None] == owner_range[None, :]).astype(jnp.int32)
    owner_ids = jnp.sum(route_hot * owners_map[None, :], axis=1)
    owner_hot = (owner_ids[:, None] == owner_range[None, :]).astype(jnp.int32)
    position = jnp.sum(owner_hot * (jnp.cumsum(owner_hot, axis=0) - 1), axis=1)
    target = owner_ids * capacity + position
    dispatch = (
        target[:, None] == jnp.arange(n_mp * capacity, dtype=jnp.int32)[None, :]
    ).astype(jnp.bfloat16)
    dispatch = relative_blocks(dispatch, 1, n_mp, me_mp)
    send_feat = (
        jnp.dot(dispatch.T, tap_store, preferred_element_type=jnp.float32)
        .astype(jnp.bfloat16)
        .reshape(n_mp, capacity, width)
    )
    items = [send_feat[0]] + [swap(send_feat[d], "mp", n_mp, d) for d in range(1, n_mp)]
    loss_scale = width / math.sqrt(row_count * n_mp)
    w_first = relative_blocks(
        lax.dynamic_index_in_dim(head_in[:, 0], sec, 0, keepdims=False), 0, n_dp, me_dp
    )
    w_second = lax.dynamic_index_in_dim(head_out[:, 0], sec, 0, keepdims=False)
    head_result = head_grads(
        jnp.concatenate(items, axis=0), w_first, w_second, loss_scale
    ).reshape(n_mp, capacity, width)
    head_cols = head_result[:, :, :col_width]
    back = [head_cols[0]] + [swap(head_cols[d], "mp", n_mp, d) for d in range(1, n_mp)]
    tap_grads = jnp.dot(
        dispatch, jnp.concatenate(back, axis=0), preferred_element_type=jnp.float32
    )

    my_cols = lambda x: x[..., :col_width]
    grad_stream = jnp.zeros((row_count, col_width), jnp.float32)
    for tick in range(n_sec):
        live = n_sec - 1 - tick
        tick_saved = saved[live]
        for slot_no in reversed(range(slot_count)):
            hit = feature_layers[live] == live * slot_count + slot_no
            grad_stream = grad_stream + jnp.where(hit, tap_grads, 0.0)
            normed, inverse, pre_act = tick_saved[slot_no]
            pre_grad = (
                grad_stream * active[slot_no] * gate_cols[slot_no] * gelu_slope(pre_act)
            ).astype(jnp.bfloat16)
            partial = jnp.dot(
                pre_grad, weights[slot_no].T, preferred_element_type=jnp.float32
            ).astype(jnp.bfloat16)
            partial = lax.optimization_barrier(partial)
            scaled = 1.0 + scale_rows[slot_no]
            row_term = jnp.sum(partial.astype(jnp.float32) * scaled * normed, axis=-1)
            pieces = [my_cols(partial)]
            terms = [row_term[None, :]]
            for d in range(1, n_dp):
                block = partial[:, d * col_width:(d + 1) * col_width]
                pairs = xor_pairs(n_dp, d, live * n_dp)
                pieces.append(lax.ppermute(block, ("section", "dp"), pairs))
                terms.append(lax.ppermute(row_term[None, :], ("section", "dp"), pairs))
            input_grad = jnp.zeros((row_count, col_width), jnp.float32)
            row_sum = jnp.zeros((row_count,), jnp.float32)
            for src in range(n_dp):
                input_grad = input_grad + pieces[src].astype(jnp.float32)
                row_sum = row_sum + terms[src][0]
            row_mean = (row_sum / width)[:, None]
            grad_stream = grad_stream + inverse * (
                input_grad * my_cols(scaled) - my_cols(normed) * row_mean
            )
        if tick + 1 < n_sec:
            sent = lax.ppermute(
                grad_stream.astype(jnp.bfloat16), "section", [(live, live - 1)]
            )
            grad_stream = sent.astype(jnp.float32)

    lat_part = student_weight.shape[1]
    latent_pre = jnp.dot(
        grad_stream.astype(jnp.bfloat16),
        lax.dynamic_slice_in_dim(patch_embed, me_dp * col_width, col_width, 1).T,
        preferred_element_type=jnp.float32,
    )
    got = [lax.dynamic_slice_in_dim(latent_pre, me_dp * lat_part, lat_part, 1)]
    for d in range(1, n_dp):
        block = lax.dynamic_slice_in_dim(latent_pre, (me_dp ^ d) * lat_part, lat_part, 1)
        got.append(lax.ppermute(block, ("section", "dp"), xor_pairs(n_dp, d, 0)))
    got = jnp.take(jnp.stack(got), me_dp ^ jnp.arange(n_dp, dtype=jnp.int32), axis=0)
    lat_sum = got[0]
    for src in range(1, n_dp):
        lat_sum = lat_sum + got[src]
    my_latent = ((1.0 - noise_level) * lat_sum).astype(jnp.bfloat16)
    if n_sec > 1:
        spread = lax.ppermute(my_latent, "section", [(0, s) for s in range(1, n_sec)])
        my_latent = jnp.where(sec == 0, my_latent, spread)

    own_rows = student_weight.shape[0]
    segment_block = width // n_sec
    hidden_cols = lax.dynamic_slice_in_dim(student_hidden, sec * segment_block, segment_block, 1)
    part_grad = lax.dot_general(
        hidden_cols, my_latent, (((0,), (0,)), ((), ())), preferred_element_type=jnp.float32
    ).reshape(n_mp, own_rows, lat_part)
    got = [lax.dynamic_index_in_dim(part_grad, me_mp, 0, keepdims=False)]
    for d in range(1, n_mp):
        outgoing = lax.dynamic_index_in_dim(part_grad, me_mp ^ d, 0, keepdims=False)
        got.append(swap(outgoing, "mp", n_mp, d))
    got = jnp.take(jnp.stack(got), me_mp ^ jnp.arange(n_mp, dtype=jnp.int32), axis=0)
    grad_sum = got[0]
    for src in range(1, n_mp):
        grad_sum = grad_sum + got[src]
    student_grad = grad_sum * width ** (-0.5)

    local_sq = jnp.sum(student_grad * student_grad).reshape(1)
    sq = gather_in_order(local_sq, "section", n_sec, sec).reshape(-1)
    sq = gather_in_order(sq, "dp", n_dp, me_dp).reshape(-1)
    sq = gather_in_order(sq, "mp", n_mp, me_mp).reshape(-1)
    total_sq = jnp.sum(sq)
    mean_square = total_sq / (width * LAT)
    student_update = student_grad * lax.rsqrt(mean_square + norm_eps)
    ema_new = ema_decay * student_ema + (1.0 - ema_decay) * (
        student_weight - step_size * student_update
    )
    return (student_update, ema_new)


def solution(mesh):
    in_specs = (
        P("mp", None),
        P(("section", "mp"), "dp"),
        P(("section", "mp"), "dp"),
        P("mp", None),
        P("mp"),
        P(),
        P("section", None, "mp", "dp"),
        P("section", None, None, None, None),
        P("section"),
        P(),
        P(None, "mp", None),
        P(),
        P(None, "mp", None, None),
        P(None, "mp", None),
    )
    out_specs = (P(("section", "mp"), "dp"), P(("section", "mp"), "dp"))
    return jax.shard_map(
        on_device, mesh=mesh, in_specs=in_specs, out_specs=out_specs, check_vma=False
    )
```

```python
import math

import jax
import jax.numpy as jnp
from jax import lax
from jax.sharding import PartitionSpec as P

D = 2432
LAT = 64


norm_eps = 1e-06
ema_decay = 0.99
step_size = 0.05


def xor_pairs(n, d, base=0):
    return [(base + i, base + (i ^ d)) for i in range(n)]


def swap(x, axis, n, d, base=0):
    return lax.ppermute(x, axis, xor_pairs(n, d, base))


def gather_in_order(x, axis, n, me, base=0):
    parts = [x] + [swap(x, axis, n, d, base) for d in range(1, n)]
    stacked = jnp.stack(parts)
    return jnp.take(stacked, me ^ jnp.arange(n, dtype=jnp.int32), axis=0)


def relative_blocks(x, axis, n, me):
    width = x.shape[axis] // n
    return jnp.concatenate(
        [lax.dynamic_slice_in_dim(x, (me ^ d) * width, width, axis) for d in range(n)], axis=axis
    )


def gelu_slope(values):
    return jax.vjp(jax.nn.gelu, values)[1](jnp.ones_like(values))[0]


def norm_back(normed, inverse, upstream):
    return inverse * (upstream - normed * jnp.mean(upstream * normed, axis=-1, keepdims=True))


def head_grads(features, w_first, w_second, loss_scale):
    feat_wide = features.astype(jnp.float32)
    inverse = lax.rsqrt(jnp.mean(feat_wide * feat_wide, axis=-1, keepdims=True) + norm_eps)
    normed = feat_wide * inverse
    hidden_pre = jnp.dot(normed.astype(jnp.bfloat16), w_first, preferred_element_type=jnp.float32)
    hidden_act = jax.nn.gelu(hidden_pre).astype(jnp.bfloat16)
    logits = jnp.dot(hidden_act, w_second, preferred_element_type=jnp.float32)
    logit_grad = -loss_scale * jax.nn.sigmoid(-logits)
    act_grad = logit_grad[:, None] * w_second.astype(jnp.float32)[None, :]
    pre_grad = (act_grad * gelu_slope(hidden_pre)).astype(jnp.bfloat16)
    normed_grad = jnp.dot(pre_grad, w_first.T, preferred_element_type=jnp.float32)
    return norm_back(normed, inverse, normed_grad).astype(jnp.bfloat16)


def on_device(
    student_hidden,
    student_weight,
    student_ema,
    noise,
    timesteps,
    patch_embed,
    teacher_weight,
    modulation,
    layer_counts,
    feature_layers,
    head_routes,
    head_owner,
    head_in,
    head_out,
):
    row_count, width = student_hidden.shape
    n_sec = lax.axis_size("section")
    n_mp = lax.axis_size("mp")
    n_dp = lax.axis_size("dp")
    sec = lax.axis_index("section")
    me_dp = lax.axis_index("dp")
    me_mp = lax.axis_index("mp")
    slot_count = teacher_weight.shape[1]
    levels = modulation.shape[2]
    col_width = width // n_dp
    samples = timesteps.shape[0]
    per_sample = row_count // samples

    t_rows = jnp.repeat(timesteps, per_sample)
    noise_level = ((t_rows + 1).astype(jnp.float32) / (levels + 1))[:, None]

    w_cols = gather_in_order(student_weight.astype(jnp.bfloat16), "dp", n_dp, me_dp)
    w_cols = jnp.concatenate(list(w_cols), axis=1)
    row_axes = ("section", "mp")
    row_me = sec * n_mp + me_mp
    w_rows = gather_in_order(w_cols, row_axes, n_sec * n_mp, row_me)
    student_full = w_rows.reshape(width, -1)
    latents = (
        jnp.dot(student_hidden, student_full, preferred_element_type=jnp.float32) * width ** (-0.5)
    ).astype(jnp.bfloat16)
    noisy_input = (
        (1.0 - noise_level) * latents.astype(jnp.float32) + noise_level * noise.astype(jnp.float32)
    ).astype(jnp.bfloat16)
    embed_rel = relative_blocks(patch_embed, 1, n_dp, me_dp)
    start_stream = jnp.dot(noisy_input, embed_rel, preferred_element_type=jnp.float32)

    weights = [
        relative_blocks(
            lax.all_gather(teacher_weight[0, slot_no], "mp", axis=0, tiled=True), 0, n_dp, me_dp
        )
        for slot_no in range(teacher_weight.shape[1])
    ]

    mod_pick = jnp.take(modulation[0], timesteps, axis=1).astype(jnp.float32)
    mod_rows = jnp.repeat(mod_pick, per_sample, axis=1)
    scale_rows = relative_blocks(mod_rows[:, :, 0, :], 2, n_dp, me_dp)
    gate_cols = lax.dynamic_slice_in_dim(mod_rows[:, :, 1, :], me_dp * col_width, col_width, 2)
    active = (jnp.arange(slot_count, dtype=jnp.int32) < layer_counts[0]).astype(jnp.float32)

    saved = []
    taps = []
    stream = start_stream
    for tick in range(n_sec):
        tick_saved = []
        tap = jnp.zeros((row_count, width), jnp.bfloat16)
        for slot_no in range(slot_count):
            inverse = lax.rsqrt(jnp.mean(stream * stream, axis=-1, keepdims=True) + norm_eps)
            normed = stream * inverse
            normed_in = (normed * (1.0 + scale_rows[slot_no])).astype(jnp.bfloat16)
            pre_act = jnp.dot(normed_in, weights[slot_no], preferred_element_type=jnp.float32)
            tick_saved.append((normed, inverse, pre_act))
            part_out = (active[slot_no] * gate_cols[slot_no] * jax.nn.gelu(pre_act)).astype(
                jnp.bfloat16
            )
            joined = [part_out] + [
                swap(part_out, ("section", "dp"), n_dp, d, base=tick * n_dp) for d in range(1, n_dp)
            ]
            joined = jnp.concatenate(joined, axis=1)
            stream = stream + joined.astype(jnp.float32)
            hit = feature_layers[tick] == tick * slot_count + slot_no
            tap = jnp.where(hit, stream.astype(jnp.bfloat16), tap)
        saved.append(tick_saved)
        taps.append(tap)
        if tick + 1 < n_sec:
            sent = lax.ppermute(stream.astype(jnp.bfloat16), "section", [(tick, tick + 1)])
            stream = sent.astype(jnp.float32)

    tap_store = taps[0]
    for tick in range(1, n_sec):
        tap_store = jnp.where(sec == tick, taps[tick], tap_store)
    capacity = 5 * row_count // (4 * n_mp)
    owner_range = jnp.arange(n_mp, dtype=jnp.int32)
    routes = lax.dynamic_index_in_dim(head_routes[:, :, 0], sec, 0, keepdims=False)
    owners_map = lax.dynamic_index_in_dim(head_owner, sec, 0, keepdims=False)
    route_hot = (routes[:, None] == owner_range[None, :]).astype(jnp.int32)
    owner_ids = jnp.sum(route_hot * owners_map[None, :], axis=1)
    owner_hot = (owner_ids[:, None] == owner_range[None, :]).astype(jnp.int32)
    position = jnp.sum(owner_hot * (jnp.cumsum(owner_hot, axis=0) - 1), axis=1)
    target = owner_ids * capacity + position
    dispatch = (
        target[:, None] == jnp.arange(n_mp * capacity, dtype=jnp.int32)[None, :]
    ).astype(jnp.bfloat16)
    dispatch = relative_blocks(dispatch, 1, n_mp, me_mp)
    send_feat = (
        jnp.dot(dispatch.T, tap_store, preferred_element_type=jnp.float32)
        .astype(jnp.bfloat16)
        .reshape(n_mp, capacity, width)
    )
    items = [send_feat[0]] + [swap(send_feat[d], "mp", n_mp, d) for d in range(1, n_mp)]
    loss_scale = width / math.sqrt(row_count * n_mp)
    w_first = relative_blocks(
        lax.dynamic_index_in_dim(head_in[:, 0], sec, 0, keepdims=False), 0, n_dp, me_dp
    )
    w_second = lax.dynamic_index_in_dim(head_out[:, 0], sec, 0, keepdims=False)
    head_result = head_grads(
        jnp.concatenate(items, axis=0), w_first, w_second, loss_scale
    ).reshape(n_mp, capacity, width)
    head_cols = head_result[:, :, :col_width]
    back = [head_cols[0]] + [swap(head_cols[d], "mp", n_mp, d) for d in range(1, n_mp)]
    tap_grads = jnp.dot(
        dispatch, jnp.concatenate(back, axis=0), preferred_element_type=jnp.float32
    )

    my_cols = lambda x: x[..., :col_width]
    grad_stream = jnp.zeros((row_count, col_width), jnp.float32)
    for tick in range(n_sec):
        live = n_sec - 1 - tick
        tick_saved = saved[live]
        for slot_no in reversed(range(slot_count)):
            hit = feature_layers[live] == live * slot_count + slot_no
            grad_stream = grad_stream + jnp.where(hit, tap_grads, 0.0)
            normed, inverse, pre_act = tick_saved[slot_no]
            pre_grad = (
                grad_stream * active[slot_no] * gate_cols[slot_no] * gelu_slope(pre_act)
            ).astype(jnp.bfloat16)
            partial = jnp.dot(
                pre_grad, weights[slot_no].T, preferred_element_type=jnp.float32
            ).astype(jnp.bfloat16)
            partial = lax.optimization_barrier(partial)
            scaled = 1.0 + scale_rows[slot_no]
            row_term = jnp.sum(partial.astype(jnp.float32) * scaled * normed, axis=-1)
            pieces = [my_cols(partial)]
            terms = [row_term[None, :]]
            for d in range(1, n_dp):
                block = partial[:, d * col_width:(d + 1) * col_width]
                pairs = xor_pairs(n_dp, d, live * n_dp)
                pieces.append(lax.ppermute(block, ("section", "dp"), pairs))
                terms.append(lax.ppermute(row_term[None, :], ("section", "dp"), pairs))
            input_grad = jnp.zeros((row_count, col_width), jnp.float32)
            row_sum = jnp.zeros((row_count,), jnp.float32)
            for src in range(n_dp):
                input_grad = input_grad + pieces[src].astype(jnp.float32)
                row_sum = row_sum + terms[src][0]
            row_mean = (row_sum / width)[:, None]
            grad_stream = grad_stream + inverse * (
                input_grad * my_cols(scaled) - my_cols(normed) * row_mean
            )
        if tick + 1 < n_sec:
            sent = lax.ppermute(
                grad_stream.astype(jnp.bfloat16), "section", [(live, live - 1)]
            )
            grad_stream = sent.astype(jnp.float32)

    lat_part = student_weight.shape[1]
    latent_pre = jnp.dot(
        grad_stream.astype(jnp.bfloat16),
        lax.dynamic_slice_in_dim(patch_embed, me_dp * col_width, col_width, 1).T,
        preferred_element_type=jnp.float32,
    )
    got = [lax.dynamic_slice_in_dim(latent_pre, me_dp * lat_part, lat_part, 1)]
    for d in range(1, n_dp):
        block = lax.dynamic_slice_in_dim(latent_pre, (me_dp ^ d) * lat_part, lat_part, 1)
        got.append(lax.ppermute(block, ("section", "dp"), xor_pairs(n_dp, d, 0)))
    lat_sum = got[0]
    for src in range(1, n_dp):
        lat_sum = lat_sum + got[src]
    my_latent = ((1.0 - noise_level) * lat_sum).astype(jnp.bfloat16)
    if n_sec > 1:
        spread = lax.ppermute(my_latent, "section", [(0, s) for s in range(1, n_sec)])
        my_latent = jnp.where(sec == 0, my_latent, spread)

    own_rows = student_weight.shape[0]
    segment_block = width // n_sec
    hidden_cols = lax.dynamic_slice_in_dim(student_hidden, sec * segment_block, segment_block, 1)
    part_grad = lax.dot_general(
        hidden_cols, my_latent, (((0,), (0,)), ((), ())), preferred_element_type=jnp.float32
    ).reshape(n_mp, own_rows, lat_part)
    got = [lax.dynamic_index_in_dim(part_grad, me_mp, 0, keepdims=False)]
    for d in range(1, n_mp):
        outgoing = lax.dynamic_index_in_dim(part_grad, me_mp ^ d, 0, keepdims=False)
        got.append(swap(outgoing, "mp", n_mp, d))
    grad_sum = got[0]
    for src in range(1, n_mp):
        grad_sum = grad_sum + got[src]
    student_grad = grad_sum * width ** (-0.5)

    local_sq = jnp.sum(student_grad * student_grad).reshape(1)
    sq = gather_in_order(local_sq, "section", n_sec, sec).reshape(-1)
    sq = gather_in_order(sq, "dp", n_dp, me_dp).reshape(-1)
    sq = gather_in_order(sq, "mp", n_mp, me_mp).reshape(-1)
    total_sq = jnp.sum(sq)
    mean_square = total_sq / (width * LAT)
    student_update = student_grad * lax.rsqrt(mean_square + norm_eps)
    ema_new = ema_decay * student_ema + (1.0 - ema_decay) * (
        student_weight - step_size * student_update
    )
    return (student_update, ema_new)


def solution(mesh):
    in_specs = (
        P("mp", None),
        P(("section", "mp"), "dp"),
        P(("section", "mp"), "dp"),
        P("mp", None),
        P("mp"),
        P(),
        P("section", None, "mp", "dp"),
        P("section", None, None, None, None),
        P("section"),
        P(),
        P(None, "mp", None),
        P(),
        P(None, "mp", None, None),
        P(None, "mp", None),
    )
    out_specs = (P(("section", "mp"), "dp"), P(("section", "mp"), "dp"))
    return jax.shard_map(
        on_device, mesh=mesh, in_specs=in_specs, out_specs=out_specs, check_vma=False
    )
```
